128 devices in a mesh: chan: 4 (over z_lo, core), blk: 32 (over z_hi, y, x).
Axes of the slice: x: 4, y: 4, z: 4 (z_hi: 2, z_lo: 2; z = z_hi * 2 + z_lo), core: 2. Of those that a mesh axis runs over, the one named last changes fastest.
Arguments:
- voltages: bfloat16 [256, 262144], P('blk', 'chan'), may hold values from -6 to 6
- fir_taps: float32 [8, 4096], replicated, may hold values from -2.1 to 2.1
Outputs:
- visibilities: float32 [2, 256, 256, 2048], P(None, 'blk', None, 'chan')
The draws below stay inside these ranges and needn't reach their ends.
All inputs are finite; a program needn't handle non-finite values.
Results may differ from the reference program's by a relative error of at most 0.0036.
Values may be sent and summed in bfloat16 or wider, within the bound.
No kernel may reach another device: no remote copies, remote signals or barrier semaphores. Data moves between devices by JAX's collectives and lax.ppermute only.
A program may use at most 192 MiB of HBM per device.

```python
import math
import jax
import jax.numpy as jnp
from jax import lax

TAPS = 8
L = 4096
C = 2048
FEEDS = 256
S = 64


def level_of(key, shape, shards, low, largest):
    gain, own = 1.0, jax.random.fold_in(key, 6)
    for dim, parts in shards:
        draws = jnp.exp(jax.random.uniform(jax.random.fold_in(own, dim), (parts,), jnp.float32, low / len(shards), largest / len(shards)))
        gain = gain * jnp.repeat(draws, shape[dim] // parts).reshape([-1 if axis == dim else 1 for axis in range(len(shape))])
    return gain


def noise(own_key, shape, deviation, most, shards=(), kind=jnp.bfloat16):
    array = deviation * jax.random.normal(own_key, shape, jnp.float32)
    if shards:
        array = array * level_of(own_key, shape, shards, -0.22, 0.18)
    return jnp.clip(array, -most, most).astype(kind)


def setup_inputs(seed: int = 0) -> dict:
    streams_of = jax.random.split(jax.random.key(seed), 3)
    return {
        "voltages": noise(streams_of[0], (FEEDS, S * L), 1.0, 6.0, ((0, 32), (1, 4))),
        "fir_taps": noise(streams_of[1], (TAPS, L), 0.35, 2.1, (), jnp.float32),
    }


def dft_table(first_channel, channel_count, length):
    channel_ids = first_channel + jnp.arange(channel_count, dtype=jnp.int32)
    sample_ids = jnp.arange(length, dtype=jnp.int32)
    phase_index = sample_ids[:, None] * channel_ids[None, :] % length
    angles = phase_index.astype(jnp.float32) * (2.0 * math.pi / length)
    normaliser = 1.0 / math.sqrt(length)
    return jnp.concatenate([jnp.cos(angles) * normaliser, -jnp.sin(angles) * normaliser], axis=1)

def reference(voltages, fir_taps):
    feed_count = voltages.shape[0]
    own_frames = voltages.reshape(feed_count, S, L)
    zero_frames = jnp.zeros((feed_count, TAPS - 1, L), voltages.dtype)
    extended = jnp.concatenate([zero_frames, own_frames], axis=1)
    filtered = jnp.zeros((feed_count, S, L), jnp.float32)
    for tap_index in range(TAPS):
        filtered = filtered + fir_taps[tap_index][None, None, :] * extended[:, tap_index:tap_index + S, :].astype(jnp.float32)
    frame_rows = filtered.reshape(feed_count * S, L)
    block_width = min(C, 512)
    pieces = []
    for first_channel in range(0, C, block_width):
        cos_sin_table = dft_table(first_channel, block_width, L)
        product = jnp.dot(frame_rows, cos_sin_table, precision=lax.Precision.HIGHEST, preferred_element_type=jnp.float32)
        pieces.append(product.reshape(feed_count * S, 2, block_width))
    spectra = jnp.concatenate(pieces, axis=2).astype(jnp.bfloat16).reshape(feed_count, S, 2, C)
    values = spectra.astype(jnp.float32)
    inverse_count = 1.0 / S
    results = []
    for first_channel in range(0, C, block_width):
        part = values[:, :, :, first_channel:first_channel + block_width]
        gram_terms = jnp.einsum('itpc,jtqc->ipjqc', part, part)
        real_part = gram_terms[:, 0, :, 0] + gram_terms[:, 1, :, 1]
        imag_part = gram_terms[:, 1, :, 0] - gram_terms[:, 0, :, 1]
        results.append(jnp.stack([real_part, imag_part]) * inverse_count)
    return jnp.concatenate(results, axis=3)
```

```python
import math

import jax
import jax.numpy as jnp
from jax import lax
from jax.experimental.layout import Layout, with_layout_constraint
from jax.sharding import PartitionSpec as P

TAPS = 8
L = 4096
C = 2048


def shifted(value, axis, steps):
    count = lax.axis_size(axis)
    leading, last = (max(0, -steps), min(count, count - steps))
    return lax.ppermute(value, axis, [(source, source + steps) for source in range(leading, last)])


def dft_table(first_channel, channel_count, length):
    channel_ids = first_channel + jnp.arange(channel_count, dtype=jnp.int32)
    sample_ids = jnp.arange(length, dtype=jnp.int32)
    phase_index = sample_ids[:, None] * channel_ids[None, :] % length
    angles = phase_index.astype(jnp.float32) * (2.0 * math.pi / length)
    normaliser = 1.0 / math.sqrt(length)
    return jnp.concatenate([jnp.cos(angles) * normaliser, -jnp.sin(angles) * normaliser], axis=1)


def correlate(own_block, every_block, inverse_count):
    real_part, imag_part = own_block[:, 0], own_block[:, 1]
    paired = jnp.stack(
        [jnp.stack([real_part, imag_part], axis=1), jnp.stack([imag_part, -real_part], axis=1)]
    )
    products = jnp.einsum(
        "riptc,jptc->rijc", paired, every_block, preferred_element_type=jnp.float32
    )
    return products * inverse_count


def on_device(voltages, fir_taps):
    feed_count = voltages.shape[0]
    frame_count = voltages.shape[1] // L
    own_frames = voltages.reshape(feed_count, frame_count, L)
    last_frames = own_frames[:, frame_count - (TAPS - 1) :, :]
    earlier = shifted(last_frames, "chan", 1)
    extended = jnp.concatenate([earlier, own_frames], axis=1)
    filtered = jnp.zeros((feed_count, frame_count, L), jnp.float32)
    for tap_index in range(TAPS):
        filtered = filtered + fir_taps[tap_index][None, None, :] * extended[
            :, tap_index : tap_index + frame_count, :
        ].astype(jnp.float32)
    frame_rows = filtered.reshape(feed_count * frame_count, L)
    block_width = min(C, 512)
    pieces = []
    for first_channel in range(0, C, block_width):
        cos_sin_table = dft_table(first_channel, block_width, L)
        product = jnp.dot(
            frame_rows,
            cos_sin_table,
            precision=lax.Precision.HIGHEST,
            preferred_element_type=jnp.float32,
        )
        pieces.append(product.reshape(feed_count * frame_count, 2, block_width))
    spectra = (
        jnp.concatenate(pieces, axis=2).astype(jnp.bfloat16).reshape(feed_count, frame_count, 2, C)
    )
    own_block = lax.all_to_all(spectra, "chan", split_axis=3, concat_axis=1, tiled=True)
    inverse_count = 1.0 / own_block.shape[1]
    own_block = own_block.transpose(0, 2, 1, 3)
    row_major = Layout(major_to_minor=tuple(range(own_block.ndim + 1)))
    local = with_layout_constraint(own_block[None], row_major)
    gathered = with_layout_constraint(
        lax.all_gather(local, "blk", axis=0, tiled=True), row_major
    )
    every_block = gathered.reshape((-1,) + own_block.shape[1:])
    return correlate(own_block, every_block, inverse_count)


def solution(mesh):
    placed = (P("blk", "chan"), P())
    return jax.shard_map(
        on_device,
        mesh=mesh,
        in_specs=placed,
        out_specs=P(None, "blk", None, "chan"),
        check_vma=False,
    )
```

```python
import math

import jax
import jax.numpy as jnp
from jax import lax
from jax.experimental.layout import Layout, with_layout_constraint
from jax.sharding import PartitionSpec as P

TAPS = 8
L = 4096
C = 2048
ROOT = 64


def shifted(value, axis, steps):
    count = lax.axis_size(axis)
    leading, last = (max(0, -steps), min(count, count - steps))
    return lax.ppermute(value, axis, [(source, source + steps) for source in range(leading, last)])


def turn(rows, columns, length):
    phase_index = jnp.arange(rows, dtype=jnp.int32)[:, None] * jnp.arange(
        columns, dtype=jnp.int32
    )[None, :] % length
    angles = phase_index.astype(jnp.float32) * (2.0 * math.pi / length)
    return jnp.cos(angles), -jnp.sin(angles)


def spectra_of(frames, groups):
    rows = frames.shape[0]
    exact = lax.Precision.HIGHEST
    first_cos, first_sin = turn(ROOT, ROOT, ROOT)
    first_table = jnp.concatenate([first_cos, first_sin], axis=1) * (1.0 / math.sqrt(L))
    split = frames.reshape(rows, ROOT, ROOT)
    stage = jnp.einsum(
        "rab,ak->rkb", split, first_table, precision=exact, preferred_element_type=jnp.float32
    )
    stage_real, stage_imag = stage[:, :ROOT], stage[:, ROOT:]
    twiddle_real, twiddle_imag = turn(ROOT, ROOT, L)
    turned_real = stage_real * twiddle_real - stage_imag * twiddle_imag
    turned_imag = stage_real * twiddle_imag + stage_imag * twiddle_real
    kept = C // ROOT
    second_cos, second_sin = turn(ROOT, kept, ROOT)
    second_table = jnp.concatenate(
        [
            jnp.concatenate([second_cos, second_sin], axis=1),
            jnp.concatenate([-second_sin, second_cos], axis=1),
        ],
        axis=0,
    )
    turned = jnp.concatenate([turned_real, turned_imag], axis=2)
    product = jnp.einsum(
        "rkb,bm->rkm", turned, second_table, precision=exact, preferred_element_type=jnp.float32
    )
    per_group = kept // groups
    product = product.reshape(rows, ROOT, 2, groups, per_group)
    return product.transpose(3, 0, 2, 4, 1).reshape(groups, rows, 2, per_group * ROOT)


def correlate(own_block, every_block, inverse_count):
    real_part, imag_part = own_block[:, :, 0], own_block[:, :, 1]
    paired = jnp.stack(
        [jnp.stack([real_part, imag_part], axis=2), jnp.stack([imag_part, -real_part], axis=2)]
    )
    blocks, feeds, spans, parts, frames, width = every_block.shape
    depth = spans * parts * frames
    left = paired.reshape(2, feeds, depth, width)
    right = every_block.reshape(blocks * feeds, depth, width)
    products = jnp.einsum("rikc,jkc->rijc", left, right, preferred_element_type=jnp.float32)
    return products * inverse_count


def on_device(voltages, fir_taps):
    feed_count = voltages.shape[0]
    frame_count = voltages.shape[1] // L
    groups = lax.axis_size("chan")
    own_frames = voltages.reshape(feed_count, frame_count, L)
    last_frames = own_frames[:, frame_count - (TAPS - 1) :, :]
    earlier = shifted(last_frames, "chan", 1)
    extended = jnp.concatenate([earlier, own_frames], axis=1)
    filtered = jnp.zeros((feed_count, frame_count, L), jnp.float32)
    for tap_index in range(TAPS):
        filtered = filtered + fir_taps[tap_index][None, None, :] * extended[
            :, tap_index : tap_index + frame_count, :
        ].astype(jnp.float32)
    frame_rows = filtered.reshape(feed_count * frame_count, L)
    spectra = spectra_of(frame_rows, groups).astype(jnp.bfloat16)
    width = spectra.shape[-1]
    spectra = spectra.reshape(groups, feed_count, frame_count, 2, width).transpose(1, 0, 3, 2, 4)
    own_block = lax.all_to_all(spectra, "chan", split_axis=1, concat_axis=1, tiled=True)
    inverse_count = 1.0 / (groups * frame_count)
    row_major = Layout(major_to_minor=tuple(range(own_block.ndim + 1)))
    local = with_layout_constraint(own_block[None], row_major)
    every_block = with_layout_constraint(
        lax.all_gather(local, "blk", axis=0, tiled=True), row_major
    )
    return correlate(own_block, every_block, inverse_count)


def solution(mesh):
    placed = (P("blk", "chan"), P())
    return jax.shard_map(
        on_device,
        mesh=mesh,
        in_specs=placed,
        out_specs=P(None, "blk", None, "chan"),
        check_vma=False,
    )
```

```python
import math

import jax
import jax.numpy as jnp
from jax import lax
from jax.experimental.layout import Layout, with_layout_constraint
from jax.sharding import PartitionSpec as P

TAPS = 8
L = 4096
C = 2048
ROOT = 64


def shifted(value, axis, steps):
    count = lax.axis_size(axis)
    leading, last = (max(0, -steps), min(count, count - steps))
    return lax.ppermute(value, axis, [(source, source + steps) for source in range(leading, last)])


def turn(rows, columns, length):
    phase_index = jnp.arange(rows, dtype=jnp.int32)[:, None] * jnp.arange(
        columns, dtype=jnp.int32
    )[None, :] % length
    angles = phase_index.astype(jnp.float32) * (2.0 * math.pi / length)
    return jnp.cos(angles), -jnp.sin(angles)


def spectra_of(frames, groups):
    rows = frames.shape[0]
    exact = lax.Precision.HIGHEST
    first_cos, first_sin = turn(ROOT, ROOT, ROOT)
    first_table = jnp.concatenate([first_cos, first_sin], axis=1) * (1.0 / math.sqrt(L))
    split = frames.reshape(rows, ROOT, ROOT)
    stage = jnp.einsum(
        "rab,ak->rkb", split, first_table, precision=exact, preferred_element_type=jnp.float32
    )
    stage_real, stage_imag = stage[:, :ROOT], stage[:, ROOT:]
    twiddle_real, twiddle_imag = turn(ROOT, ROOT, L)
    turned_real = stage_real * twiddle_real - stage_imag * twiddle_imag
    turned_imag = stage_real * twiddle_imag + stage_imag * twiddle_real
    kept = C // ROOT
    second_cos, second_sin = turn(ROOT, kept, ROOT)
    second_table = jnp.concatenate(
        [
            jnp.concatenate([second_cos, second_sin], axis=1),
            jnp.concatenate([-second_sin, second_cos], axis=1),
        ],
        axis=0,
    )
    turned = jnp.concatenate([turned_real, turned_imag], axis=2)
    product = jnp.einsum(
        "rkb,bm->rkm", turned, second_table, precision=exact, preferred_element_type=jnp.float32
    )
    per_group = kept // groups
    product = product.reshape(rows, ROOT, 2, groups, per_group)
    return product.transpose(3, 0, 2, 4, 1).reshape(groups, rows, 2, per_group * ROOT)


def correlate(own_block, every_block, inverse_count):
    real_part, imag_part = own_block[:, :, :, 0], own_block[:, :, :, 1]
    paired = jnp.stack(
        [jnp.stack([real_part, imag_part], axis=3), jnp.stack([imag_part, -real_part], axis=3)]
    )
    blocks, feeds, width, depth = every_block.shape
    left = paired.reshape(2, feeds, width, depth)
    right = every_block.reshape(blocks * feeds, width, depth)
    products = jnp.einsum("rick,jck->rijc", left, right, preferred_element_type=jnp.float32)
    return products * inverse_count


def on_device(voltages, fir_taps):
    feed_count = voltages.shape[0]
    frame_count = voltages.shape[1] // L
    groups = lax.axis_size("chan")
    own_frames = voltages.reshape(feed_count, frame_count, L)
    last_frames = own_frames[:, frame_count - (TAPS - 1) :, :]
    earlier = shifted(last_frames, "chan", 1)
    extended = jnp.concatenate([earlier, own_frames], axis=1)
    filtered = jnp.zeros((feed_count, frame_count, L), jnp.float32)
    for tap_index in range(TAPS):
        filtered = filtered + fir_taps[tap_index][None, None, :] * extended[
            :, tap_index : tap_index + frame_count, :
        ].astype(jnp.float32)
    frame_rows = filtered.reshape(feed_count * frame_count, L)
    spectra = spectra_of(frame_rows, groups).astype(jnp.bfloat16)
    width = spectra.shape[-1]
    spectra = spectra.reshape(groups, feed_count, frame_count, 2, width).transpose(1, 0, 3, 2, 4)
    own_block = lax.all_to_all(spectra, "chan", split_axis=1, concat_axis=1, tiled=True)
    inverse_count = 1.0 / (groups * frame_count)
    feeds, spans, parts, frames, width = own_block.shape
    own_block = own_block.transpose(0, 4, 1, 2, 3)
    local = own_block.reshape(1, feeds, width, spans * parts * frames)
    row_major = Layout(major_to_minor=tuple(range(local.ndim)))
    local = with_layout_constraint(local, row_major)
    every_block = with_layout_constraint(
        lax.all_gather(local, "blk", axis=0, tiled=True), row_major
    )
    return correlate(own_block, every_block, inverse_count)


def solution(mesh):
    placed = (P("blk", "chan"), P())
    return jax.shard_map(
        on_device,
        mesh=mesh,
        in_specs=placed,
        out_specs=P(None, "blk", None, "chan"),
        check_vma=False,
    )
```

```python
import math

import jax
import jax.numpy as jnp
from jax import lax
from jax.experimental.layout import Layout, with_layout_constraint
from jax.sharding import PartitionSpec as P

TAPS = 8
L = 4096
C = 2048
ROOT = 64


def shifted(value, axis, steps):
    count = lax.axis_size(axis)
    leading, last = (max(0, -steps), min(count, count - steps))
    return lax.ppermute(value, axis, [(source, source + steps) for source in range(leading, last)])


def turn(rows, columns, length):
    phase_index = jnp.arange(rows, dtype=jnp.int32)[:, None] * jnp.arange(
        columns, dtype=jnp.int32
    )[None, :] % length
    angles = phase_index.astype(jnp.float32) * (2.0 * math.pi / length)
    return jnp.cos(angles), -jnp.sin(angles)


def spectra_of(frames, groups):
    rows = frames.shape[0]
    exact = lax.Precision.HIGHEST
    first_cos, first_sin = turn(ROOT, ROOT, ROOT)
    first_table = jnp.concatenate([first_cos, first_sin], axis=1) * (1.0 / math.sqrt(L))
    split = frames.reshape(rows, ROOT, ROOT)
    stage = jnp.einsum(
        "rab,ak->rkb", split, first_table, precision=exact, preferred_element_type=jnp.float32
    )
    stage_real, stage_imag = stage[:, :ROOT], stage[:, ROOT:]
    twiddle_real, twiddle_imag = turn(ROOT, ROOT, L)
    turned_real = stage_real * twiddle_real - stage_imag * twiddle_imag
    turned_imag = stage_real * twiddle_imag + stage_imag * twiddle_real
    kept = C // ROOT
    second_cos, second_sin = turn(ROOT, kept, ROOT)
    second_table = jnp.concatenate(
        [
            jnp.concatenate([second_cos, second_sin], axis=1),
            jnp.concatenate([-second_sin, second_cos], axis=1),
        ],
        axis=0,
    )
    turned = jnp.concatenate([turned_real, turned_imag], axis=2)
    product = jnp.einsum(
        "rkb,bm->rkm", turned, second_table, precision=exact, preferred_element_type=jnp.float32
    )
    per_group = kept // groups
    product = product.reshape(rows, ROOT, 2, groups, per_group)
    return product.transpose(3, 0, 2, 4, 1).reshape(groups, rows, 2, per_group * ROOT)


def correlate(own_block, every_block, inverse_count):
    real_part, imag_part = own_block[:, :, :, 0], own_block[:, :, :, 1]
    paired = jnp.stack(
        [jnp.stack([real_part, imag_part], axis=3), jnp.stack([imag_part, -real_part], axis=3)]
    )
    blocks, feeds, width, depth = every_block.shape
    left = paired.reshape(2, feeds, width, depth)
    right = every_block.reshape(blocks * feeds, width, depth)
    products = jnp.einsum("rick,jck->rijc", left, right, preferred_element_type=jnp.float32)
    return products * inverse_count


def on_device(voltages, fir_taps):
    feed_count = voltages.shape[0]
    frame_count = voltages.shape[1] // L
    groups = lax.axis_size("chan")
    own_frames = voltages.reshape(feed_count, frame_count, L)
    last_frames = own_frames[:, frame_count - (TAPS - 1) :, :]
    earlier = shifted(last_frames, "chan", 1)
    extended = jnp.concatenate([earlier, own_frames], axis=1)
    filtered = jnp.zeros((feed_count, frame_count, L), jnp.float32)
    for tap_index in range(TAPS):
        filtered = filtered + fir_taps[tap_index][None, None, :] * extended[
            :, tap_index : tap_index + frame_count, :
        ].astype(jnp.float32)
    frame_rows = filtered.reshape(feed_count * frame_count, L)
    spectra = spectra_of(frame_rows, groups).astype(jnp.bfloat16)
    width = spectra.shape[-1]
    spectra = spectra.reshape(groups, feed_count, frame_count, 2, width).transpose(1, 0, 3, 2, 4)
    own_block = lax.all_to_all(spectra, "chan", split_axis=1, concat_axis=1, tiled=True)
    inverse_count = 1.0 / (groups * frame_count)
    feeds, spans, parts, frames, width = own_block.shape
    own_block = own_block.transpose(0, 4, 1, 2, 3)
    local = own_block.reshape(1, feeds, width, spans * parts * frames)
    row_major = Layout(major_to_minor=tuple(range(local.ndim)))
    pieces = []
    piece_width = width // 2
    for first in range(0, width, piece_width):
        piece = with_layout_constraint(local[:, :, first : first + piece_width], row_major)
        every_piece = with_layout_constraint(
            lax.all_gather(piece, "blk", axis=0, tiled=True), row_major
        )
        pieces.append(
            correlate(own_block[:, first : first + piece_width], every_piece, inverse_count)
        )
    return jnp.concatenate(pieces, axis=3)


def solution(mesh):
    placed = (P("blk", "chan"), P())
    return jax.shard_map(
        on_device,
        mesh=mesh,
        in_specs=placed,
        out_specs=P(None, "blk", None, "chan"),
        check_vma=False,
    )
```

```python
import math

import jax
import jax.numpy as jnp
from jax import lax
from jax.experimental.layout import Layout, with_layout_constraint
from jax.sharding import PartitionSpec as P

TAPS = 8
L = 4096
C = 2048
ROOT = 64


def shifted(value, axis, steps):
    count = lax.axis_size(axis)
    leading, last = (max(0, -steps), min(count, count - steps))
    return lax.ppermute(value, axis, [(source, source + steps) for source in range(leading, last)])


def turn(rows, columns, length):
    phase_index = jnp.arange(rows, dtype=jnp.int32)[:, None] * jnp.arange(
        columns, dtype=jnp.int32
    )[None, :] % length
    angles = phase_index.astype(jnp.float32) * (2.0 * math.pi / length)
    return jnp.cos(angles), -jnp.sin(angles)


def spectra_of(frames, groups):
    rows = frames.shape[0]
    exact = lax.Precision.HIGHEST
    first_cos, first_sin = turn(ROOT, ROOT, ROOT)
    first_table = jnp.concatenate([first_cos, first_sin], axis=1) * (1.0 / math.sqrt(L))
    split = frames.reshape(rows, ROOT, ROOT)
    stage = jnp.einsum(
        "rab,ak->rkb", split, first_table, precision=exact, preferred_element_type=jnp.float32
    )
    stage_real, stage_imag = stage[:, :ROOT], stage[:, ROOT:]
    twiddle_real, twiddle_imag = turn(ROOT, ROOT, L)
    turned_real = stage_real * twiddle_real - stage_imag * twiddle_imag
    turned_imag = stage_real * twiddle_imag + stage_imag * twiddle_real
    kept = C // ROOT
    second_cos, second_sin = turn(ROOT, kept, ROOT)
    second_table = jnp.concatenate(
        [
            jnp.concatenate([second_cos, second_sin], axis=1),
            jnp.concatenate([-second_sin, second_cos], axis=1),
        ],
        axis=0,
    )
    turned = jnp.concatenate([turned_real, turned_imag], axis=2)
    product = jnp.einsum(
        "rkb,bm->rkm", turned, second_table, precision=exact, preferred_element_type=jnp.float32
    )
    per_group = kept // groups
    product = product.reshape(rows, ROOT, 2, groups, per_group)
    return product.transpose(3, 0, 2, 4, 1).reshape(groups, rows, 2, per_group * ROOT)


def correlate(own_block, every_block, inverse_count):
    real_part, imag_part = own_block[:, :, :, 0], own_block[:, :, :, 1]
    paired = jnp.stack(
        [jnp.stack([real_part, imag_part], axis=3), jnp.stack([imag_part, -real_part], axis=3)]
    )
    blocks, feeds, width, depth = every_block.shape
    left = paired.reshape(2, feeds, width, depth)
    right = every_block.reshape(blocks * feeds, width, depth)
    products = jnp.einsum("rick,jck->rijc", left, right, preferred_element_type=jnp.float32)
    return products * inverse_count


def corner_turn(spectra, axis):
    count = lax.axis_size(axis)
    me = lax.axis_index(axis)
    pieces = []
    for steps in range(count):
        outgoing = lax.dynamic_index_in_dim(spectra, (me + steps) % count, axis=1, keepdims=False)
        if steps:
            outgoing = lax.ppermute(
                outgoing, axis, [(source, (source + steps) % count) for source in range(count)]
            )
        pieces.append(outgoing)
    return jnp.stack(pieces, axis=1)


def on_device(voltages, fir_taps):
    feed_count = voltages.shape[0]
    frame_count = voltages.shape[1] // L
    groups = lax.axis_size("chan")
    own_frames = voltages.reshape(feed_count, frame_count, L)
    last_frames = own_frames[:, frame_count - (TAPS - 1) :, :]
    earlier = shifted(last_frames, "chan", 1)
    extended = jnp.concatenate([earlier, own_frames], axis=1)
    filtered = jnp.zeros((feed_count, frame_count, L), jnp.float32)
    for tap_index in range(TAPS):
        filtered = filtered + fir_taps[tap_index][None, None, :] * extended[
            :, tap_index : tap_index + frame_count, :
        ].astype(jnp.float32)
    frame_rows = filtered.reshape(feed_count * frame_count, L)
    spectra = spectra_of(frame_rows, groups).astype(jnp.bfloat16)
    width = spectra.shape[-1]
    spectra = spectra.reshape(groups, feed_count, frame_count, 2, width).transpose(1, 0, 3, 2, 4)
    own_block = corner_turn(spectra, "chan")
    inverse_count = 1.0 / (groups * frame_count)
    feeds, spans, parts, frames, width = own_block.shape
    own_block = own_block.transpose(0, 4, 1, 2, 3)
    local = own_block.reshape(1, feeds, width, spans * parts * frames)
    row_major = Layout(major_to_minor=tuple(range(local.ndim)))
    local = with_layout_constraint(local, row_major)
    every_block = with_layout_constraint(
        lax.all_gather(local, "blk", axis=0, tiled=True), row_major
    )
    return correlate(own_block, every_block, inverse_count)


def solution(mesh):
    placed = (P("blk", "chan"), P())
    return jax.shard_map(
        on_device,
        mesh=mesh,
        in_specs=placed,
        out_specs=P(None, "blk", None, "chan"),
        check_vma=False,
    )
```

```python
import math

import jax
import jax.numpy as jnp
from jax import lax
from jax.experimental.layout import Layout, with_layout_constraint
from jax.sharding import PartitionSpec as P

TAPS = 8
L = 4096
C = 2048
ROOT = 64
CHAN = ("z_lo", "core")
PLANE = "z_hi"
WITHIN = ("y", "x")
BLK = (PLANE,) + WITHIN


def shifted(value, axis, steps):
    count = lax.axis_size(axis)
    leading, last = (max(0, -steps), min(count, count - steps))
    return lax.ppermute(value, axis, [(source, source + steps) for source in range(leading, last)])


def turn(rows, columns, length):
    phase_index = jnp.arange(rows, dtype=jnp.int32)[:, None] * jnp.arange(
        columns, dtype=jnp.int32
    )[None, :] % length
    angles = phase_index.astype(jnp.float32) * (2.0 * math.pi / length)
    return jnp.cos(angles), -jnp.sin(angles)


def spectra_of(frames, groups):
    rows = frames.shape[0]
    exact = lax.Precision.HIGHEST
    first_cos, first_sin = turn(ROOT, ROOT, ROOT)
    first_table = jnp.concatenate([first_cos, first_sin], axis=1) * (1.0 / math.sqrt(L))
    split = frames.reshape(rows, ROOT, ROOT)
    stage = jnp.einsum(
        "rab,ak->rkb", split, first_table, precision=exact, preferred_element_type=jnp.float32
    )
    stage_real, stage_imag = stage[:, :ROOT], stage[:, ROOT:]
    twiddle_real, twiddle_imag = turn(ROOT, ROOT, L)
    turned_real = stage_real * twiddle_real - stage_imag * twiddle_imag
    turned_imag = stage_real * twiddle_imag + stage_imag * twiddle_real
    kept = C // ROOT
    second_cos, second_sin = turn(ROOT, kept, ROOT)
    second_table = jnp.concatenate(
        [
            jnp.concatenate([second_cos, second_sin], axis=1),
            jnp.concatenate([-second_sin, second_cos], axis=1),
        ],
        axis=0,
    )
    turned = jnp.concatenate([turned_real, turned_imag], axis=2)
    product = jnp.einsum(
        "rkb,bm->rkm", turned, second_table, precision=exact, preferred_element_type=jnp.float32
    )
    per_group = kept // groups
    product = product.reshape(rows, ROOT, 2, groups, per_group)
    return product.transpose(3, 0, 2, 4, 1).reshape(groups, rows, 2, per_group * ROOT)


def correlate(own_block, every_block, inverse_count):
    real_part, imag_part = own_block[:, :, :, 0], own_block[:, :, :, 1]
    paired = jnp.stack(
        [jnp.stack([real_part, imag_part], axis=3), jnp.stack([imag_part, -real_part], axis=3)]
    )
    blocks, feeds, width, depth = every_block.shape
    left = paired.reshape(2, feeds, width, depth)
    right = every_block.reshape(blocks * feeds, width, depth)
    products = jnp.einsum("rick,jck->rijc", left, right, preferred_element_type=jnp.float32)
    return products * inverse_count


def corner_turn(spectra, axis):
    count = lax.axis_size(axis)
    me = lax.axis_index(axis)
    pieces = []
    for steps in range(count):
        outgoing = lax.dynamic_index_in_dim(spectra, (me + steps) % count, axis=1, keepdims=False)
        if steps:
            outgoing = lax.ppermute(
                outgoing, axis, [(source, (source + steps) % count) for source in range(count)]
            )
        pieces.append(outgoing)
    return jnp.stack(pieces, axis=1)


def on_device(voltages, fir_taps):
    feed_count = voltages.shape[0]
    frame_count = voltages.shape[1] // L
    groups = lax.axis_size(CHAN)
    own_frames = voltages.reshape(feed_count, frame_count, L)
    last_frames = own_frames[:, frame_count - (TAPS - 1) :, :]
    earlier = shifted(last_frames, CHAN, 1)
    extended = jnp.concatenate([earlier, own_frames], axis=1)
    filtered = jnp.zeros((feed_count, frame_count, L), jnp.float32)
    for tap_index in range(TAPS):
        filtered = filtered + fir_taps[tap_index][None, None, :] * extended[
            :, tap_index : tap_index + frame_count, :
        ].astype(jnp.float32)
    frame_rows = filtered.reshape(feed_count * frame_count, L)
    spectra = spectra_of(frame_rows, groups).astype(jnp.bfloat16)
    width = spectra.shape[-1]
    spectra = spectra.reshape(groups, feed_count, frame_count, 2, width).transpose(1, 0, 3, 2, 4)
    own_block = corner_turn(spectra, CHAN)
    inverse_count = 1.0 / (groups * frame_count)
    feeds, spans, parts, frames, width = own_block.shape
    own_block = own_block.transpose(0, 4, 1, 2, 3)
    local = own_block.reshape(1, feeds, width, spans * parts * frames)
    row_major = Layout(major_to_minor=tuple(range(local.ndim + 1)))
    partner = lax.ppermute(local, PLANE, [(0, 1), (1, 0)])
    first_plane = lax.axis_index(PLANE) == 0
    pair = jnp.where(
        first_plane,
        jnp.concatenate([local, partner], axis=0),
        jnp.concatenate([partner, local], axis=0),
    )
    pair = with_layout_constraint(pair[None], row_major)
    gathered = with_layout_constraint(
        lax.all_gather(pair, WITHIN, axis=0, tiled=True), row_major
    )
    every_block = gathered.reshape((-1,) + local.shape[1:])
    products = correlate(own_block, every_block, inverse_count)
    parts, feeds, _, width = products.shape
    products = products.reshape(parts, feeds, gathered.shape[0], 2, feeds, width)
    return products.transpose(0, 1, 3, 2, 4, 5).reshape(parts, feeds, -1, width)


def solution(mesh):
    chan_axes, blk_axes = mesh.devices.shape
    split = jax.sharding.Mesh(
        mesh.devices.reshape(2, chan_axes // 2, 2, 4, blk_axes // 8), CHAN + BLK
    )
    placed = (P(BLK, CHAN), P())
    return jax.shard_map(
        on_device,
        mesh=split,
        in_specs=placed,
        out_specs=P(None, BLK, None, CHAN),
        check_vma=False,
    )
```

```python
import math

import jax
import jax.numpy as jnp
from jax import lax
from jax.experimental.layout import Layout, with_layout_constraint
from jax.sharding import PartitionSpec as P

TAPS = 8
L = 4096
C = 2048
ROOT = 64
CHAN = ("z_lo", "core")
PLANE = "z_hi"
WITHIN = ("y", "x")
BLK = (PLANE,) + WITHIN


def shifted(value, axis, steps):
    count = lax.axis_size(axis)
    leading, last = (max(0, -steps), min(count, count - steps))
    return lax.ppermute(value, axis, [(source, source + steps) for source in range(leading, last)])


def turn(rows, columns, length):
    phase_index = jnp.arange(rows, dtype=jnp.int32)[:, None] * jnp.arange(
        columns, dtype=jnp.int32
    )[None, :] % length
    angles = phase_index.astype(jnp.float32) * (2.0 * math.pi / length)
    return jnp.cos(angles), -jnp.sin(angles)


def spectra_of(frames, groups):
    rows = frames.shape[0]
    exact = lax.Precision.HIGHEST
    first_cos, first_sin = turn(ROOT, ROOT, ROOT)
    first_table = jnp.concatenate([first_cos, first_sin], axis=1) * (1.0 / math.sqrt(L))
    split = frames.reshape(rows, ROOT, ROOT)
    stage = jnp.einsum(
        "rab,ak->rkb", split, first_table, precision=exact, preferred_element_type=jnp.float32
    )
    stage_real, stage_imag = stage[:, :ROOT], stage[:, ROOT:]
    twiddle_real, twiddle_imag = turn(ROOT, ROOT, L)
    turned_real = stage_real * twiddle_real - stage_imag * twiddle_imag
    turned_imag = stage_real * twiddle_imag + stage_imag * twiddle_real
    kept = C // ROOT
    second_cos, second_sin = turn(ROOT, kept, ROOT)
    second_table = jnp.concatenate(
        [
            jnp.concatenate([second_cos, second_sin], axis=1),
            jnp.concatenate([-second_sin, second_cos], axis=1),
        ],
        axis=0,
    )
    turned = jnp.concatenate([turned_real, turned_imag], axis=2)
    product = jnp.einsum(
        "rkb,bm->rkm", turned, second_table, precision=exact, preferred_element_type=jnp.float32
    )
    per_group = kept // groups
    product = product.reshape(rows, ROOT, 2, groups, per_group)
    return product.transpose(3, 0, 2, 4, 1).reshape(groups, rows, 2, per_group * ROOT)


def correlate(own_block, every_block, inverse_count):
    real_part, imag_part = own_block[:, :, :, 0], own_block[:, :, :, 1]
    paired = jnp.stack(
        [jnp.stack([real_part, imag_part], axis=3), jnp.stack([imag_part, -real_part], axis=3)]
    )
    left = paired.reshape((2,) + own_block.shape[:2] + (-1,))
    products = jnp.einsum("rick,jck->rijc", left, every_block, preferred_element_type=jnp.float32)
    return products * inverse_count


def corner_turn(spectra):
    count = lax.axis_size(CHAN)
    me = lax.axis_index(CHAN)
    planes = []
    for flip in range(2):
        pieces = []
        for steps in range(count):
            outgoing = lax.dynamic_index_in_dim(
                spectra, (me + steps) % count, axis=1, keepdims=False
            )
            if steps or flip:
                pairs = [
                    (source * 2 + plane, ((source + steps) % count) * 2 + (plane ^ flip))
                    for source in range(count)
                    for plane in range(2)
                ]
                outgoing = lax.ppermute(outgoing, CHAN + (PLANE,), pairs)
            pieces.append(outgoing)
        planes.append(jnp.stack(pieces, axis=1))
    return planes


def on_device(voltages, fir_taps):
    feed_count = voltages.shape[0]
    frame_count = voltages.shape[1] // L
    groups = lax.axis_size(CHAN)
    own_frames = voltages.reshape(feed_count, frame_count, L)
    last_frames = own_frames[:, frame_count - (TAPS - 1) :, :]
    earlier = shifted(last_frames, CHAN, 1)
    extended = jnp.concatenate([earlier, own_frames], axis=1)
    filtered = jnp.zeros((feed_count, frame_count, L), jnp.float32)
    for tap_index in range(TAPS):
        filtered = filtered + fir_taps[tap_index][None, None, :] * extended[
            :, tap_index : tap_index + frame_count, :
        ].astype(jnp.float32)
    frame_rows = filtered.reshape(feed_count * frame_count, L)
    spectra = spectra_of(frame_rows, groups).astype(jnp.bfloat16)
    width = spectra.shape[-1]
    spectra = spectra.reshape(groups, feed_count, frame_count, 2, width).transpose(1, 0, 3, 2, 4)
    own_block, partner_block = corner_turn(spectra)
    inverse_count = 1.0 / (groups * frame_count)
    feeds, spans, parts, frames, width = own_block.shape

    own_block = own_block.transpose(0, 4, 1, 2, 3)
    partner_block = partner_block.transpose(0, 4, 1, 2, 3)
    row_major = Layout(major_to_minor=tuple(range(5)))
    first_plane = lax.axis_index(PLANE) == 0
    pair = jnp.where(
        first_plane,
        jnp.stack([own_block, partner_block]),
        jnp.stack([partner_block, own_block]),
    )
    pair = with_layout_constraint(
        pair.reshape(2, 1, feeds, width, spans * parts * frames), row_major
    )
    gathered = with_layout_constraint(
        lax.all_gather(pair, WITHIN, axis=1, tiled=True), row_major
    )
    every_block = gathered.reshape((-1,) + gathered.shape[3:])
    return correlate(own_block, every_block, inverse_count)


def solution(mesh):
    chan_axes, blk_axes = mesh.devices.shape
    split = jax.sharding.Mesh(
        mesh.devices.reshape(2, chan_axes // 2, 2, 4, blk_axes // 8), CHAN + BLK
    )
    placed = (P(BLK, CHAN), P())
    return jax.shard_map(
        on_device,
        mesh=split,
        in_specs=placed,
        out_specs=P(None, BLK, None, CHAN),
        check_vma=False,
    )
```

```python
import math

import jax
import jax.numpy as jnp
from jax import lax
from jax.experimental.layout import Layout, with_layout_constraint
from jax.sharding import PartitionSpec as P

TAPS = 8
L = 4096
C = 2048
ROOT = 64
CHAN = ("z_lo", "core")
PLANE = "z_hi"
WITHIN = ("y", "x")
BLK = (PLANE,) + WITHIN


def shifted(value, axis, steps):
    count = lax.axis_size(axis)
    leading, last = (max(0, -steps), min(count, count - steps))
    return lax.ppermute(value, axis, [(source, source + steps) for source in range(leading, last)])


def turn(rows, columns, length):
    phase_index = jnp.arange(rows, dtype=jnp.int32)[:, None] * jnp.arange(
        columns, dtype=jnp.int32
    )[None, :] % length
    angles = phase_index.astype(jnp.float32) * (2.0 * math.pi / length)
    return jnp.cos(angles), -jnp.sin(angles)


def spectra_of(frames, groups):
    rows = frames.shape[0]
    exact = lax.Precision.HIGHEST
    first_cos, first_sin = turn(ROOT, ROOT, ROOT)
    first_table = jnp.concatenate([first_cos, first_sin], axis=1) * (1.0 / math.sqrt(L))
    split = frames.reshape(rows, ROOT, ROOT)
    stage = jnp.einsum(
        "rab,ak->rkb", split, first_table, precision=exact, preferred_element_type=jnp.float32
    )
    stage_real, stage_imag = stage[:, :ROOT], stage[:, ROOT:]
    twiddle_real, twiddle_imag = turn(ROOT, ROOT, L)
    turned_real = stage_real * twiddle_real - stage_imag * twiddle_imag
    turned_imag = stage_real * twiddle_imag + stage_imag * twiddle_real
    kept = C // ROOT
    second_cos, second_sin = turn(ROOT, kept, ROOT)
    second_table = jnp.concatenate(
        [
            jnp.concatenate([second_cos, second_sin], axis=1),
            jnp.concatenate([-second_sin, second_cos], axis=1),
        ],
        axis=0,
    )
    turned = jnp.concatenate([turned_real, turned_imag], axis=2)
    product = jnp.einsum(
        "rkb,bm->rkm", turned, second_table, precision=exact, preferred_element_type=jnp.float32
    )
    per_group = kept // groups
    product = product.reshape(rows, ROOT, 2, groups, per_group)
    return product.transpose(3, 0, 2, 4, 1).reshape(groups, rows, 2, per_group * ROOT)


def correlate(own_block, every_block, inverse_count):
    real_part, imag_part = own_block[:, :, :, 0], own_block[:, :, :, 1]
    paired = jnp.stack(
        [jnp.stack([real_part, imag_part], axis=3), jnp.stack([imag_part, -real_part], axis=3)]
    )
    left = paired.reshape((2,) + own_block.shape[:2] + (-1,))
    products = jnp.einsum("rick,jck->rijc", left, every_block, preferred_element_type=jnp.float32)
    return products * inverse_count


def corner_turn(spectra):
    count = lax.axis_size(CHAN)
    me = lax.axis_index(CHAN)
    planes = []
    for flip in range(2):
        pieces = []
        for steps in range(count):
            outgoing = lax.dynamic_index_in_dim(
                spectra, (me + steps) % count, axis=1, keepdims=False
            )
            if steps or flip:
                pairs = [
                    (source * 2 + plane, ((source + steps) % count) * 2 + (plane ^ flip))
                    for source in range(count)
                    for plane in range(2)
                ]
                outgoing = lax.ppermute(outgoing, CHAN + (PLANE,), pairs)
            pieces.append(outgoing)
        planes.append(jnp.stack(pieces, axis=1))
    return planes


def on_device(voltages, fir_taps):
    feed_count = voltages.shape[0]
    frame_count = voltages.shape[1] // L
    groups = lax.axis_size(CHAN)
    own_frames = voltages.reshape(feed_count, frame_count, L)
    last_frames = own_frames[:, frame_count - (TAPS - 1) :, :]
    earlier = shifted(last_frames, CHAN, 1)
    extended = jnp.concatenate([earlier, own_frames], axis=1)
    filtered = jnp.zeros((feed_count, frame_count, L), jnp.float32)
    for tap_index in range(TAPS):
        filtered = filtered + fir_taps[tap_index][None, None, :] * extended[
            :, tap_index : tap_index + frame_count, :
        ].astype(jnp.float32)
    frame_rows = filtered.reshape(feed_count * frame_count, L)
    spectra = spectra_of(frame_rows, groups).astype(jnp.bfloat16)
    width = spectra.shape[-1]
    spectra = spectra.reshape(groups, feed_count, frame_count, 2, width).transpose(1, 0, 3, 2, 4)
    own_block, partner_block = corner_turn(spectra)
    inverse_count = 1.0 / (groups * frame_count)
    feeds, spans, parts, frames, width = own_block.shape

    own_block = own_block.transpose(0, 4, 1, 2, 3)
    partner_block = partner_block.transpose(0, 4, 1, 2, 3)
    row_major = Layout(major_to_minor=tuple(range(4)))
    local = with_layout_constraint(
        own_block.reshape(1, feeds, width, spans * parts * frames), row_major
    )
    gathered = with_layout_constraint(
        lax.all_gather(local, WITHIN, axis=0, tiled=True), row_major
    )
    plane_blocks = gathered.reshape((-1,) + gathered.shape[2:])
    partner_part = correlate(partner_block, plane_blocks, inverse_count)
    other_part = lax.ppermute(partner_part, PLANE, [(0, 1), (1, 0)])
    own_part = correlate(own_block, plane_blocks, inverse_count)
    first_plane = lax.axis_index(PLANE) == 0
    return jnp.where(
        first_plane,
        jnp.concatenate([own_part, other_part], axis=2),
        jnp.concatenate([other_part, own_part], axis=2),
    )


def solution(mesh):
    chan_axes, blk_axes = mesh.devices.shape
    split = jax.sharding.Mesh(
        mesh.devices.reshape(2, chan_axes // 2, 2, 4, blk_axes // 8), CHAN + BLK
    )
    placed = (P(BLK, CHAN), P())
    return jax.shard_map(
        on_device,
        mesh=split,
        in_specs=placed,
        out_specs=P(None, BLK, None, CHAN),
        check_vma=False,
    )
```

```python
import math

import jax
import jax.numpy as jnp
from jax import lax
from jax.experimental.layout import Layout, with_layout_constraint
from jax.sharding import PartitionSpec as P

TAPS = 8
L = 4096
C = 2048
ROOT = 64
CHAN = ("z_lo", "core")
PLANE = "z_hi"
WITHIN = ("y", "x")
BLK = (PLANE,) + WITHIN


def shifted(value, axis, steps):
    count = lax.axis_size(axis)
    leading, last = (max(0, -steps), min(count, count - steps))
    return lax.ppermute(value, axis, [(source, source + steps) for source in range(leading, last)])


def turn(rows, columns, length):
    phase_index = jnp.arange(rows, dtype=jnp.int32)[:, None] * jnp.arange(
        columns, dtype=jnp.int32
    )[None, :] % length
    angles = phase_index.astype(jnp.float32) * (2.0 * math.pi / length)
    return jnp.cos(angles), -jnp.sin(angles)


def spectra_of(frames, groups):
    rows = frames.shape[0]
    exact = lax.Precision.HIGHEST
    first_cos, first_sin = turn(ROOT, ROOT, ROOT)
    first_table = jnp.concatenate([first_cos, first_sin], axis=1) * (1.0 / math.sqrt(L))
    split = frames.reshape(rows, ROOT, ROOT)
    stage = jnp.einsum(
        "rab,ak->rkb", split, first_table, precision=exact, preferred_element_type=jnp.float32
    )
    stage_real, stage_imag = stage[:, :ROOT], stage[:, ROOT:]
    twiddle_real, twiddle_imag = turn(ROOT, ROOT, L)
    turned_real = stage_real * twiddle_real - stage_imag * twiddle_imag
    turned_imag = stage_real * twiddle_imag + stage_imag * twiddle_real
    kept = C // ROOT
    second_cos, second_sin = turn(ROOT, kept, ROOT)
    second_table = jnp.concatenate(
        [
            jnp.concatenate([second_cos, second_sin], axis=1),
            jnp.concatenate([-second_sin, second_cos], axis=1),
        ],
        axis=0,
    )
    turned = jnp.concatenate([turned_real, turned_imag], axis=2)
    product = jnp.einsum(
        "rkb,bm->rkm", turned, second_table, precision=exact, preferred_element_type=jnp.float32
    )
    per_group = kept // groups
    product = product.reshape(rows, ROOT, 2, groups, per_group)
    return product.transpose(3, 0, 2, 4, 1).reshape(groups, rows, 2, per_group * ROOT)


def correlate(own_block, every_block, inverse_count):
    real_part, imag_part = own_block[:, :, :, 0], own_block[:, :, :, 1]
    paired = jnp.stack(
        [jnp.stack([real_part, imag_part], axis=3), jnp.stack([imag_part, -real_part], axis=3)]
    )
    left = paired.reshape((2,) + own_block.shape[:2] + (-1,))
    products = jnp.einsum("rick,jck->rijc", left, every_block, preferred_element_type=jnp.float32)
    return products * inverse_count


def corner_turn(spectra):
    count = lax.axis_size(CHAN)
    me = lax.axis_index(CHAN)
    planes = []
    for flip in range(2):
        pieces = []
        for steps in range(count):
            outgoing = lax.dynamic_index_in_dim(
                spectra, (me + steps) % count, axis=1, keepdims=False
            )
            if steps or flip:
                pairs = [
                    (source * 2 + plane, ((source + steps) % count) * 2 + (plane ^ flip))
                    for source in range(count)
                    for plane in range(2)
                ]
                outgoing = lax.ppermute(outgoing, CHAN + (PLANE,), pairs)
            pieces.append(outgoing)
        planes.append(jnp.stack(pieces, axis=1))
    return planes


def on_device(voltages, fir_taps):
    feed_count = voltages.shape[0]
    frame_count = voltages.shape[1] // L
    groups = lax.axis_size(CHAN)
    own_frames = voltages.reshape(feed_count, frame_count, L)
    last_frames = own_frames[:, frame_count - (TAPS - 1) :, :]
    earlier = shifted(last_frames, CHAN, 1)
    extended = jnp.concatenate([earlier, own_frames], axis=1)
    filtered = jnp.zeros((feed_count, frame_count, L), jnp.float32)
    for tap_index in range(TAPS):
        filtered = filtered + fir_taps[tap_index][None, None, :] * extended[
            :, tap_index : tap_index + frame_count, :
        ].astype(jnp.float32)
    frame_rows = filtered.reshape(feed_count * frame_count, L)
    spectra = spectra_of(frame_rows, groups).astype(jnp.bfloat16)
    width = spectra.shape[-1]
    spectra = spectra.reshape(groups, feed_count, frame_count, 2, width).transpose(1, 0, 3, 2, 4)
    own_block, partner_block = corner_turn(spectra)
    inverse_count = 1.0 / (groups * frame_count)
    feeds, spans, parts, frames, width = own_block.shape

    own_block = own_block.transpose(0, 4, 1, 2, 3)
    partner_block = partner_block.transpose(0, 4, 1, 2, 3)
    row_major = Layout(major_to_minor=tuple(range(4)))
    local = with_layout_constraint(
        own_block.reshape(1, feeds, width, spans * parts * frames), row_major
    )
    gathered = with_layout_constraint(
        lax.all_gather(local, WITHIN, axis=0, tiled=True), row_major
    )
    plane_blocks = gathered.reshape((-1,) + gathered.shape[2:])
    partner_part = correlate(partner_block, plane_blocks, inverse_count)
    other_part = lax.ppermute(partner_part, PLANE, [(0, 1), (1, 0)])
    own_part = correlate(own_block, plane_blocks, inverse_count)
    plane = lax.axis_index(PLANE)
    span = own_part.shape[2]
    whole = jnp.zeros(own_part.shape[:2] + (2 * span,) + own_part.shape[3:], own_part.dtype)
    whole = lax.dynamic_update_slice_in_dim(whole, own_part, plane * span, axis=2)
    return lax.dynamic_update_slice_in_dim(whole, other_part, (1 - plane) * span, axis=2)


def solution(mesh):
    chan_axes, blk_axes = mesh.devices.shape
    split = jax.sharding.Mesh(
        mesh.devices.reshape(2, chan_axes // 2, 2, 4, blk_axes // 8), CHAN + BLK
    )
    placed = (P(BLK, CHAN), P())
    return jax.shard_map(
        on_device,
        mesh=split,
        in_specs=placed,
        out_specs=P(None, BLK, None, CHAN),
        check_vma=False,
    )
```

```python
import math

import jax
import jax.numpy as jnp
from jax import lax
from jax.experimental.layout import Layout, with_layout_constraint
from jax.sharding import PartitionSpec as P

TAPS = 8
L = 4096
C = 2048
ROOT = 64
CHAN = ("z_lo", "core")
PLANE = "z_hi"
WITHIN = ("y", "x")
BLK = (PLANE,) + WITHIN


def shifted(value, axis, steps):
    count = lax.axis_size(axis)
    leading, last = (max(0, -steps), min(count, count - steps))
    return lax.ppermute(value, axis, [(source, source + steps) for source in range(leading, last)])


def turn(rows, columns, length):
    phase_index = jnp.arange(rows, dtype=jnp.int32)[:, None] * jnp.arange(
        columns, dtype=jnp.int32
    )[None, :] % length
    angles = phase_index.astype(jnp.float32) * (2.0 * math.pi / length)
    return jnp.cos(angles), -jnp.sin(angles)


def spectra_of(frames, groups):
    rows = frames.shape[0]
    exact = lax.Precision.HIGHEST
    first_cos, first_sin = turn(ROOT, ROOT, ROOT)
    first_table = jnp.concatenate([first_cos, first_sin], axis=1) * (1.0 / math.sqrt(L))
    split = frames.reshape(rows, ROOT, ROOT)
    stage = jnp.einsum(
        "rab,ak->rkb", split, first_table, precision=exact, preferred_element_type=jnp.float32
    )
    stage_real, stage_imag = stage[:, :ROOT], stage[:, ROOT:]
    twiddle_real, twiddle_imag = turn(ROOT, ROOT, L)
    turned_real = stage_real * twiddle_real - stage_imag * twiddle_imag
    turned_imag = stage_real * twiddle_imag + stage_imag * twiddle_real
    kept = C // ROOT
    second_cos, second_sin = turn(ROOT, kept, ROOT)
    second_table = jnp.concatenate(
        [
            jnp.concatenate([second_cos, second_sin], axis=1),
            jnp.concatenate([-second_sin, second_cos], axis=1),
        ],
        axis=0,
    )
    turned = jnp.concatenate([turned_real, turned_imag], axis=2)
    product = jnp.einsum(
        "rkb,bm->rkm", turned, second_table, precision=exact, preferred_element_type=jnp.float32
    )
    per_group = kept // groups
    product = product.reshape(rows, ROOT, 2, groups, per_group)
    return product.transpose(3, 0, 2, 4, 1).reshape(groups, rows, 2, per_group * ROOT)


def correlate(own_block, every_block, inverse_count):
    real_part, imag_part = own_block[:, :, :, 0], own_block[:, :, :, 1]
    paired = jnp.stack(
        [jnp.stack([real_part, imag_part], axis=3), jnp.stack([imag_part, -real_part], axis=3)]
    )
    left = paired.reshape((2,) + own_block.shape[:2] + (-1,))
    products = jnp.einsum("rick,jck->rijc", left, every_block, preferred_element_type=jnp.float32)
    return products * inverse_count


def corner_turn(spectra):
    count = lax.axis_size(CHAN)
    me = lax.axis_index(CHAN)
    planes = []
    for flip in range(2):
        pieces = []
        for steps in range(count):
            outgoing = lax.dynamic_index_in_dim(
                spectra, (me + steps) % count, axis=1, keepdims=False
            )
            if steps or flip:
                pairs = [
                    (source * 2 + plane, ((source + steps) % count) * 2 + (plane ^ flip))
                    for source in range(count)
                    for plane in range(2)
                ]
                outgoing = lax.ppermute(outgoing, CHAN + (PLANE,), pairs)
            pieces.append(outgoing)
        planes.append(jnp.stack(pieces, axis=1))
    return planes


def on_device(voltages, fir_taps):
    feed_count = voltages.shape[0]
    frame_count = voltages.shape[1] // L
    groups = lax.axis_size(CHAN)
    own_frames = voltages.reshape(feed_count, frame_count, L)
    last_frames = own_frames[:, frame_count - (TAPS - 1) :, :]
    earlier = shifted(last_frames, CHAN, 1)
    extended = jnp.concatenate([earlier, own_frames], axis=1)
    filtered = jnp.zeros((feed_count, frame_count, L), jnp.float32)
    for tap_index in range(TAPS):
        filtered = filtered + fir_taps[tap_index][None, None, :] * extended[
            :, tap_index : tap_index + frame_count, :
        ].astype(jnp.float32)
    frame_rows = filtered.reshape(feed_count * frame_count, L)
    spectra = spectra_of(frame_rows, groups).astype(jnp.bfloat16)
    width = spectra.shape[-1]
    spectra = spectra.reshape(groups, feed_count, frame_count, 2, width).transpose(1, 0, 3, 2, 4)
    own_block, partner_block = corner_turn(spectra)
    inverse_count = 1.0 / (groups * frame_count)
    feeds, spans, parts, frames, width = own_block.shape

    own_block = own_block.transpose(0, 4, 1, 2, 3)
    partner_block = partner_block.transpose(0, 4, 1, 2, 3)
    row_major = Layout(major_to_minor=tuple(range(4)))
    local = with_layout_constraint(
        own_block.reshape(1, feeds, width, spans * parts * frames), row_major
    )
    gathered = with_layout_constraint(
        lax.all_gather(local, WITHIN, axis=0, tiled=True), row_major
    )
    plane_blocks = gathered.reshape((-1,) + gathered.shape[2:])
    others = []
    half = width // 2
    for first in (0, half):
        partner_part = correlate(
            partner_block[:, first : first + half], plane_blocks[:, first : first + half],
            inverse_count,
        )
        others.append(lax.ppermute(partner_part, PLANE, [(0, 1), (1, 0)]))
    own_part = correlate(own_block, plane_blocks, inverse_count)
    plane = lax.axis_index(PLANE)
    span = own_part.shape[2]
    whole = jnp.zeros(own_part.shape[:2] + (2 * span,) + own_part.shape[3:], own_part.dtype)
    whole = lax.dynamic_update_slice_in_dim(whole, own_part, plane * span, axis=2)
    for index, other_part in enumerate(others):
        whole = lax.dynamic_update_slice(
            whole, other_part, (0, 0, (1 - plane) * span, index * half)
        )
    return whole


def solution(mesh):
    chan_axes, blk_axes = mesh.devices.shape
    split = jax.sharding.Mesh(
        mesh.devices.reshape(2, chan_axes // 2, 2, 4, blk_axes // 8), CHAN + BLK
    )
    placed = (P(BLK, CHAN), P())
    return jax.shard_map(
        on_device,
        mesh=split,
        in_specs=placed,
        out_specs=P(None, BLK, None, CHAN),
        check_vma=False,
    )
```

```python
import math

import jax
import jax.numpy as jnp
from jax import lax
from jax.experimental.layout import Layout, with_layout_constraint
from jax.sharding import PartitionSpec as P

TAPS = 8
L = 4096
C = 2048
ROOT = 64
CHAN = ("z_lo", "core")
PLANE = "z_hi"
WITHIN = ("y", "x")
BLK = (PLANE,) + WITHIN


def shifted(value, axis, steps):
    count = lax.axis_size(axis)
    leading, last = (max(0, -steps), min(count, count - steps))
    return lax.ppermute(value, axis, [(source, source + steps) for source in range(leading, last)])


def turn(rows, columns, length):
    phase_index = jnp.arange(rows, dtype=jnp.int32)[:, None] * jnp.arange(
        columns, dtype=jnp.int32
    )[None, :] % length
    angles = phase_index.astype(jnp.float32) * (2.0 * math.pi / length)
    return jnp.cos(angles), -jnp.sin(angles)


def spectra_of(frames, groups):
    rows = frames.shape[0]
    exact = lax.Precision.HIGHEST
    first_cos, first_sin = turn(ROOT, ROOT, ROOT)
    first_table = jnp.concatenate([first_cos, first_sin], axis=1) * (1.0 / math.sqrt(L))
    split = frames.reshape(rows, ROOT, ROOT)
    stage = jnp.einsum(
        "rab,ak->rkb", split, first_table, precision=exact, preferred_element_type=jnp.float32
    )
    stage_real, stage_imag = stage[:, :ROOT], stage[:, ROOT:]
    twiddle_real, twiddle_imag = turn(ROOT, ROOT, L)
    turned_real = stage_real * twiddle_real - stage_imag * twiddle_imag
    turned_imag = stage_real * twiddle_imag + stage_imag * twiddle_real
    kept = C // ROOT
    second_cos, second_sin = turn(ROOT, kept, ROOT)
    second_table = jnp.concatenate(
        [
            jnp.concatenate([second_cos, second_sin], axis=1),
            jnp.concatenate([-second_sin, second_cos], axis=1),
        ],
        axis=0,
    )
    turned = jnp.concatenate([turned_real, turned_imag], axis=2)
    product = jnp.einsum(
        "rkb,bm->rkm", turned, second_table, precision=exact, preferred_element_type=jnp.float32
    )
    per_group = kept // groups
    product = product.reshape(rows, ROOT, 2, groups, per_group)
    return product.transpose(3, 0, 2, 4, 1).reshape(groups, rows, 2, per_group * ROOT)


def correlate(own_block, every_block, inverse_count):
    real_part, imag_part = own_block[:, :, :, 0], own_block[:, :, :, 1]
    paired = jnp.stack(
        [jnp.stack([real_part, imag_part], axis=3), jnp.stack([imag_part, -real_part], axis=3)]
    )
    left = paired.reshape((2,) + own_block.shape[:2] + (-1,))
    products = jnp.einsum("rick,jck->rijc", left, every_block, preferred_element_type=jnp.float32)
    return products * inverse_count


def corner_turn(spectra):
    count = lax.axis_size(CHAN)
    me = lax.axis_index(CHAN)
    planes = []
    for flip in range(2):
        pieces = []
        for steps in range(count):
            outgoing = lax.dynamic_index_in_dim(
                spectra, (me + steps) % count, axis=1, keepdims=False
            )
            if steps or flip:
                pairs = [
                    (source * 2 + plane, ((source + steps) % count) * 2 + (plane ^ flip))
                    for source in range(count)
                    for plane in range(2)
                ]
                outgoing = lax.ppermute(outgoing, CHAN + (PLANE,), pairs)
            pieces.append(outgoing)
        planes.append(jnp.stack(pieces, axis=1))
    return planes


def on_device(voltages, fir_taps):
    feed_count = voltages.shape[0]
    frame_count = voltages.shape[1] // L
    groups = lax.axis_size(CHAN)
    own_frames = voltages.reshape(feed_count, frame_count, L)
    last_frames = own_frames[:, frame_count - (TAPS - 1) :, :]
    earlier = shifted(last_frames, CHAN, 1)
    extended = jnp.concatenate([earlier, own_frames], axis=1)
    filtered = jnp.zeros((feed_count, frame_count, L), jnp.float32)
    for tap_index in range(TAPS):
        filtered = filtered + fir_taps[tap_index][None, None, :] * extended[
            :, tap_index : tap_index + frame_count, :
        ].astype(jnp.float32)
    frame_rows = filtered.reshape(feed_count * frame_count, L)
    spectra = spectra_of(frame_rows, groups).astype(jnp.bfloat16)
    width = spectra.shape[-1]
    spectra = spectra.reshape(groups, feed_count, frame_count, 2, width).transpose(1, 0, 3, 2, 4)
    own_block, partner_block = corner_turn(spectra)
    inverse_count = 1.0 / (groups * frame_count)
    feeds, spans, parts, frames, width = own_block.shape

    own_block = own_block.transpose(0, 4, 1, 2, 3)
    partner_block = partner_block.transpose(0, 4, 1, 2, 3)
    row_major = Layout(major_to_minor=tuple(range(4)))
    local = with_layout_constraint(
        own_block.reshape(1, feeds, width, spans * parts * frames), row_major
    )
    gathered = with_layout_constraint(
        lax.all_gather(local, WITHIN, axis=0, tiled=True), row_major
    )
    plane_blocks = gathered.reshape((-1,) + gathered.shape[2:])
    others = []
    half = width // 4
    for first in range(0, width, half):
        partner_part = correlate(
            partner_block[:, first : first + half], plane_blocks[:, first : first + half],
            inverse_count,
        )
        others.append(lax.ppermute(partner_part, PLANE, [(0, 1), (1, 0)]))
    own_part = correlate(own_block, plane_blocks, inverse_count)
    plane = lax.axis_index(PLANE)
    span = own_part.shape[2]
    whole = jnp.zeros(own_part.shape[:2] + (2 * span,) + own_part.shape[3:], own_part.dtype)
    whole = lax.dynamic_update_slice_in_dim(whole, own_part, plane * span, axis=2)
    for index, other_part in enumerate(others):
        whole = lax.dynamic_update_slice(
            whole, other_part, (0, 0, (1 - plane) * span, index * half)
        )
    return whole


def solution(mesh):
    chan_axes, blk_axes = mesh.devices.shape
    split = jax.sharding.Mesh(
        mesh.devices.reshape(2, chan_axes // 2, 2, 4, blk_axes // 8), CHAN + BLK
    )
    placed = (P(BLK, CHAN), P())
    return jax.shard_map(
        on_device,
        mesh=split,
        in_specs=placed,
        out_specs=P(None, BLK, None, CHAN),
        check_vma=False,
    )
```

```python
import math

import jax
import jax.numpy as jnp
from jax import lax
from jax.experimental.layout import Layout, with_layout_constraint
from jax.sharding import PartitionSpec as P

TAPS = 8
L = 4096
C = 2048
ROOT = 64
CHAN = ("z_lo", "core")
PLANE = "z_hi"
WITHIN = ("y", "x")
BLK = (PLANE,) + WITHIN


def shifted(value, axis, steps):
    count = lax.axis_size(axis)
    leading, last = (max(0, -steps), min(count, count - steps))
    return lax.ppermute(value, axis, [(source, source + steps) for source in range(leading, last)])


def turn(rows, columns, length):
    phase_index = jnp.arange(rows, dtype=jnp.int32)[:, None] * jnp.arange(
        columns, dtype=jnp.int32
    )[None, :] % length
    angles = phase_index.astype(jnp.float32) * (2.0 * math.pi / length)
    return jnp.cos(angles), -jnp.sin(angles)


def spectra_of(frames, groups):
    rows = frames.shape[0]
    exact = lax.Precision.HIGHEST
    first_cos, first_sin = turn(ROOT, ROOT, ROOT)
    first_table = jnp.concatenate([first_cos, first_sin], axis=1) * (1.0 / math.sqrt(L))
    split = frames.reshape(rows, ROOT, ROOT)
    stage = jnp.einsum(
        "rab,ak->rkb", split, first_table, precision=exact, preferred_element_type=jnp.float32
    )
    stage_real, stage_imag = stage[:, :ROOT], stage[:, ROOT:]
    twiddle_real, twiddle_imag = turn(ROOT, ROOT, L)
    turned_real = stage_real * twiddle_real - stage_imag * twiddle_imag
    turned_imag = stage_real * twiddle_imag + stage_imag * twiddle_real
    kept = C // ROOT
    second_cos, second_sin = turn(ROOT, kept, ROOT)
    second_table = jnp.concatenate(
        [
            jnp.concatenate([second_cos, second_sin], axis=1),
            jnp.concatenate([-second_sin, second_cos], axis=1),
        ],
        axis=0,
    )
    turned = jnp.concatenate([turned_real, turned_imag], axis=2)
    product = jnp.einsum(
        "rkb,bm->rkm", turned, second_table, precision=exact, preferred_element_type=jnp.float32
    )
    per_group = kept // groups
    product = product.reshape(rows, ROOT, 2, groups, per_group)
    return product.transpose(3, 0, 2, 4, 1).reshape(groups, rows, 2, per_group * ROOT)


def correlate(own_block, every_block, inverse_count):
    real_part, imag_part = own_block[:, :, :, 0], own_block[:, :, :, 1]
    paired = jnp.stack(
        [jnp.stack([real_part, imag_part], axis=3), jnp.stack([imag_part, -real_part], axis=3)]
    )
    left = paired.reshape((2,) + own_block.shape[:2] + (-1,))
    products = jnp.einsum("rick,jck->rijc", left, every_block, preferred_element_type=jnp.float32)
    return products * inverse_count


def corner_turn(spectra):
    count = lax.axis_size(CHAN)
    me = lax.axis_index(CHAN)
    planes = []
    for flip in range(2):
        pieces = []
        for steps in range(count):
            outgoing = lax.dynamic_index_in_dim(
                spectra, (me + steps) % count, axis=1, keepdims=False
            )
            if steps or flip:
                pairs = [
                    (source * 2 + plane, ((source + steps) % count) * 2 + (plane ^ flip))
                    for source in range(count)
                    for plane in range(2)
                ]
                outgoing = lax.ppermute(outgoing, CHAN + (PLANE,), pairs)
            pieces.append(outgoing)
        planes.append(jnp.stack(pieces, axis=1))
    return planes


def on_device(voltages, fir_taps):
    feed_count = voltages.shape[0]
    frame_count = voltages.shape[1] // L
    groups = lax.axis_size(CHAN)
    own_frames = voltages.reshape(feed_count, frame_count, L)
    last_frames = own_frames[:, frame_count - (TAPS - 1) :, :]
    earlier = shifted(last_frames, CHAN, 1)
    extended = jnp.concatenate([earlier, own_frames], axis=1)
    filtered = jnp.zeros((feed_count, frame_count, L), jnp.float32)
    for tap_index in range(TAPS):
        filtered = filtered + fir_taps[tap_index][None, None, :] * extended[
            :, tap_index : tap_index + frame_count, :
        ].astype(jnp.float32)
    frame_rows = filtered.reshape(feed_count * frame_count, L)
    spectra = spectra_of(frame_rows, groups).astype(jnp.bfloat16)
    width = spectra.shape[-1]
    spectra = spectra.reshape(groups, feed_count, frame_count, 2, width).transpose(1, 0, 3, 2, 4)
    own_block, partner_block = corner_turn(spectra)
    inverse_count = 1.0 / (groups * frame_count)
    feeds, spans, parts, frames, width = own_block.shape

    own_block = own_block.transpose(0, 4, 1, 2, 3)
    partner_block = partner_block.transpose(0, 4, 1, 2, 3)
    row_major = Layout(major_to_minor=tuple(range(4)))
    half = width // 2
    owns, others = [], []
    for first in (0, half):
        local = with_layout_constraint(
            own_block[:, first : first + half].reshape(1, feeds, half, spans * parts * frames),
            row_major,
        )
        gathered = with_layout_constraint(
            lax.all_gather(local, WITHIN, axis=0, tiled=True), row_major
        )
        plane_blocks = gathered.reshape((-1,) + gathered.shape[2:])
        partner_part = correlate(
            partner_block[:, first : first + half], plane_blocks, inverse_count
        )
        others.append(lax.ppermute(partner_part, PLANE, [(0, 1), (1, 0)]))
        owns.append(correlate(own_block[:, first : first + half], plane_blocks, inverse_count))
    plane = lax.axis_index(PLANE)
    span = plane_blocks.shape[0]
    whole = jnp.zeros((2, feeds, 2 * span, width), jnp.float32)
    for index in range(2):
        whole = lax.dynamic_update_slice(whole, owns[index], (0, 0, plane * span, index * half))
        whole = lax.dynamic_update_slice(
            whole, others[index], (0, 0, (1 - plane) * span, index * half)
        )
    return whole


def solution(mesh):
    chan_axes, blk_axes = mesh.devices.shape
    split = jax.sharding.Mesh(
        mesh.devices.reshape(2, chan_axes // 2, 2, 4, blk_axes // 8), CHAN + BLK
    )
    placed = (P(BLK, CHAN), P())
    return jax.shard_map(
        on_device,
        mesh=split,
        in_specs=placed,
        out_specs=P(None, BLK, None, CHAN),
        check_vma=False,
    )
```

```python
import math

import jax
import jax.numpy as jnp
from jax import lax
from jax.experimental.layout import Layout, with_layout_constraint
from jax.sharding import PartitionSpec as P

TAPS = 8
L = 4096
C = 2048
ROOT = 64
CHAN = ("z_lo", "core")
PLANE = "z_hi"
WITHIN = ("y", "x")
BLK = (PLANE,) + WITHIN


def shifted(value, axis, steps):
    count = lax.axis_size(axis)
    leading, last = (max(0, -steps), min(count, count - steps))
    return lax.ppermute(value, axis, [(source, source + steps) for source in range(leading, last)])


def turn(rows, columns, length):
    phase_index = jnp.arange(rows, dtype=jnp.int32)[:, None] * jnp.arange(
        columns, dtype=jnp.int32
    )[None, :] % length
    angles = phase_index.astype(jnp.float32) * (2.0 * math.pi / length)
    return jnp.cos(angles), -jnp.sin(angles)


def spectra_of(frames, groups):
    rows = frames.shape[0]
    exact = lax.Precision.HIGHEST
    first_cos, first_sin = turn(ROOT, ROOT, ROOT)
    first_table = jnp.concatenate([first_cos, first_sin], axis=1) * (1.0 / math.sqrt(L))
    split = frames.reshape(rows, ROOT, ROOT)
    stage = jnp.einsum(
        "rab,ak->rkb", split, first_table, precision=exact, preferred_element_type=jnp.float32
    )
    stage_real, stage_imag = stage[:, :ROOT], stage[:, ROOT:]
    twiddle_real, twiddle_imag = turn(ROOT, ROOT, L)
    turned_real = stage_real * twiddle_real - stage_imag * twiddle_imag
    turned_imag = stage_real * twiddle_imag + stage_imag * twiddle_real
    kept = C // ROOT
    second_cos, second_sin = turn(ROOT, kept, ROOT)
    second_table = jnp.concatenate(
        [
            jnp.concatenate([second_cos, second_sin], axis=1),
            jnp.concatenate([-second_sin, second_cos], axis=1),
        ],
        axis=0,
    )
    turned = jnp.concatenate([turned_real, turned_imag], axis=2)
    product = jnp.einsum(
        "rkb,bm->rkm", turned, second_table, precision=exact, preferred_element_type=jnp.float32
    )
    per_group = kept // groups
    product = product.reshape(rows, ROOT, 2, groups, per_group)
    return product.transpose(3, 0, 2, 4, 1).reshape(groups, rows, 2, per_group * ROOT)


def correlate(own_block, every_block, inverse_count):
    real_part, imag_part = own_block[:, :, :, 0], own_block[:, :, :, 1]
    paired = jnp.stack(
        [jnp.stack([real_part, imag_part], axis=3), jnp.stack([imag_part, -real_part], axis=3)]
    )
    left = paired.reshape((2,) + own_block.shape[:2] + (-1,))
    products = jnp.einsum("rick,jck->rijc", left, every_block, preferred_element_type=jnp.float32)
    return products * inverse_count


def corner_turn(spectra):
    count = lax.axis_size(CHAN)
    me = lax.axis_index(CHAN)
    planes = []
    for flip in range(2):
        pieces = []
        for steps in range(count):
            outgoing = lax.dynamic_index_in_dim(
                spectra, (me + steps) % count, axis=1, keepdims=False
            )
            if steps or flip:
                pairs = [
                    (source * 2 + plane, ((source + steps) % count) * 2 + (plane ^ flip))
                    for source in range(count)
                    for plane in range(2)
                ]
                outgoing = lax.ppermute(outgoing, CHAN + (PLANE,), pairs)
            pieces.append(outgoing)
        planes.append(jnp.stack(pieces, axis=1))
    return planes


def on_device(voltages, fir_taps):
    feed_count = voltages.shape[0]
    frame_count = voltages.shape[1] // L
    groups = lax.axis_size(CHAN)
    own_frames = voltages.reshape(feed_count, frame_count, L)
    last_frames = own_frames[:, frame_count - (TAPS - 1) :, :]
    earlier = shifted(last_frames, CHAN, 1)
    extended = jnp.concatenate([earlier, own_frames], axis=1)
    filtered = jnp.zeros((feed_count, frame_count, L), jnp.float32)
    for tap_index in range(TAPS):
        filtered = filtered + fir_taps[tap_index][None, None, :] * extended[
            :, tap_index : tap_index + frame_count, :
        ].astype(jnp.float32)
    frame_rows = filtered.reshape(feed_count * frame_count, L)
    spectra = spectra_of(frame_rows, groups).astype(jnp.bfloat16)
    width = spectra.shape[-1]
    spectra = spectra.reshape(groups, feed_count, frame_count, 2, width).transpose(1, 0, 3, 2, 4)
    own_block, partner_block = corner_turn(spectra)
    inverse_count = 1.0 / (groups * frame_count)
    feeds, spans, parts, frames, width = own_block.shape

    own_block = own_block.transpose(0, 4, 1, 2, 3)
    partner_block = partner_block.transpose(0, 4, 1, 2, 3)
    row_major = Layout(major_to_minor=tuple(range(4)))
    half = width // 2
    owns, others, sent = [], [], []
    for first in (0, half):
        local = with_layout_constraint(
            own_block[:, first : first + half].reshape(1, feeds, half, spans * parts * frames),
            row_major,
        )
        gathered = with_layout_constraint(
            lax.all_gather(local, WITHIN, axis=0, tiled=True), row_major
        )
        plane_blocks = gathered.reshape((-1,) + gathered.shape[2:])
        if owns:
            plane_blocks, owns[0], _ = lax.optimization_barrier(
                (plane_blocks, owns[0], sent[0])
            )
        partner_part = correlate(
            partner_block[:, first : first + half], plane_blocks, inverse_count
        )
        sent.append(partner_part)
        others.append(lax.ppermute(partner_part, PLANE, [(0, 1), (1, 0)]))
        owns.append(correlate(own_block[:, first : first + half], plane_blocks, inverse_count))
    plane = lax.axis_index(PLANE)
    span = plane_blocks.shape[0]
    whole = jnp.zeros((2, feeds, 2 * span, width), jnp.float32)
    for index in range(2):
        whole = lax.dynamic_update_slice(whole, owns[index], (0, 0, plane * span, index * half))
        whole = lax.dynamic_update_slice(
            whole, others[index], (0, 0, (1 - plane) * span, index * half)
        )
    return whole


def solution(mesh):
    chan_axes, blk_axes = mesh.devices.shape
    split = jax.sharding.Mesh(
        mesh.devices.reshape(2, chan_axes // 2, 2, 4, blk_axes // 8), CHAN + BLK
    )
    placed = (P(BLK, CHAN), P())
    return jax.shard_map(
        on_device,
        mesh=split,
        in_specs=placed,
        out_specs=P(None, BLK, None, CHAN),
        check_vma=False,
    )
```

```python
import math

import jax
import jax.numpy as jnp
from jax import lax
from jax.experimental.layout import Layout, with_layout_constraint
from jax.sharding import PartitionSpec as P

TAPS = 8
L = 4096
C = 2048
ROOT = 64
CHAN = ("z_lo", "core")
PLANE = "z_hi"
WITHIN = ("y", "x")
BLK = (PLANE,) + WITHIN


def shifted(value, axis, steps):
    count = lax.axis_size(axis)
    leading, last = (max(0, -steps), min(count, count - steps))
    return lax.ppermute(value, axis, [(source, source + steps) for source in range(leading, last)])


def turn(rows, columns, length):
    phase_index = jnp.arange(rows, dtype=jnp.int32)[:, None] * jnp.arange(
        columns, dtype=jnp.int32
    )[None, :] % length
    angles = phase_index.astype(jnp.float32) * (2.0 * math.pi / length)
    return jnp.cos(angles), -jnp.sin(angles)


def spectra_of(frames, groups):
    rows = frames.shape[0]
    exact = lax.Precision.HIGHEST
    first_cos, first_sin = turn(ROOT, ROOT, ROOT)
    first_table = jnp.concatenate([first_cos, first_sin], axis=1) * (1.0 / math.sqrt(L))
    split = frames.reshape(rows, ROOT, ROOT)
    stage = jnp.einsum(
        "rab,ak->rkb", split, first_table, precision=exact, preferred_element_type=jnp.float32
    )
    stage_real, stage_imag = stage[:, :ROOT], stage[:, ROOT:]
    twiddle_real, twiddle_imag = turn(ROOT, ROOT, L)
    turned_real = stage_real * twiddle_real - stage_imag * twiddle_imag
    turned_imag = stage_real * twiddle_imag + stage_imag * twiddle_real
    kept = C // ROOT
    second_cos, second_sin = turn(ROOT, kept, ROOT)
    second_table = jnp.concatenate(
        [
            jnp.concatenate([second_cos, second_sin], axis=1),
            jnp.concatenate([-second_sin, second_cos], axis=1),
        ],
        axis=0,
    )
    turned = jnp.concatenate([turned_real, turned_imag], axis=2)
    product = jnp.einsum(
        "rkb,bm->rkm", turned, second_table, precision=exact, preferred_element_type=jnp.float32
    )
    per_group = kept // groups
    product = product.reshape(rows, ROOT, 2, groups, per_group)
    return product.transpose(3, 0, 2, 4, 1).reshape(groups, rows, 2, per_group * ROOT)


def correlate(own_block, every_block, inverse_count):
    real_part, imag_part = own_block[:, :, :, 0], own_block[:, :, :, 1]
    paired = jnp.stack(
        [jnp.stack([real_part, imag_part], axis=3), jnp.stack([imag_part, -real_part], axis=3)]
    )
    left = paired.reshape((2,) + own_block.shape[:2] + (-1,))
    products = jnp.einsum("rick,jck->rijc", left, every_block, preferred_element_type=jnp.float32)
    return products * inverse_count


def corner_turn(spectra):
    count = lax.axis_size(CHAN)
    me = lax.axis_index(CHAN)
    planes = []
    for flip in range(2):
        pieces = []
        for steps in range(count):
            outgoing = lax.dynamic_index_in_dim(
                spectra, (me + steps) % count, axis=1, keepdims=False
            )
            if steps or flip:
                pairs = [
                    (source * 2 + plane, ((source + steps) % count) * 2 + (plane ^ flip))
                    for source in range(count)
                    for plane in range(2)
                ]
                outgoing = lax.ppermute(outgoing, CHAN + (PLANE,), pairs)
            pieces.append(outgoing)
        planes.append(jnp.stack(pieces, axis=1))
    return planes


def on_device(voltages, fir_taps):
    feed_count = voltages.shape[0]
    frame_count = voltages.shape[1] // L
    groups = lax.axis_size(CHAN)
    own_frames = voltages.reshape(feed_count, frame_count, L)
    last_frames = own_frames[:, frame_count - (TAPS - 1) :, :]
    earlier = shifted(last_frames, CHAN, 1)
    extended = jnp.concatenate([earlier, own_frames], axis=1)
    filtered = jnp.zeros((feed_count, frame_count, L), jnp.float32)
    for tap_index in range(TAPS):
        filtered = filtered + fir_taps[tap_index][None, None, :] * extended[
            :, tap_index : tap_index + frame_count, :
        ].astype(jnp.float32)
    frame_rows = filtered.reshape(feed_count * frame_count, L)
    spectra = spectra_of(frame_rows, groups).astype(jnp.bfloat16)
    width = spectra.shape[-1]
    spectra = spectra.reshape(groups, feed_count, frame_count, 2, width).transpose(1, 0, 3, 2, 4)
    own_block, partner_block = corner_turn(spectra)
    inverse_count = 1.0 / (groups * frame_count)
    feeds, spans, parts, frames, width = own_block.shape

    own_block = own_block.transpose(0, 4, 1, 2, 3)
    partner_block = partner_block.transpose(0, 4, 1, 2, 3)
    row_major = Layout(major_to_minor=tuple(range(4)))
    split = width * 5 // 8
    spans_of = [(0, split), (split, width - split)]
    owns, others, sent = [], [], []
    for first, half in spans_of:
        local = with_layout_constraint(
            own_block[:, first : first + half].reshape(1, feeds, half, spans * parts * frames),
            row_major,
        )
        gathered = with_layout_constraint(
            lax.all_gather(local, WITHIN, axis=0, tiled=True), row_major
        )
        plane_blocks = gathered.reshape((-1,) + gathered.shape[2:])
        if owns:
            plane_blocks, owns[0], _ = lax.optimization_barrier(
                (plane_blocks, owns[0], sent[0])
            )
        partner_part = correlate(
            partner_block[:, first : first + half], plane_blocks, inverse_count
        )
        sent.append(partner_part)
        others.append(lax.ppermute(partner_part, PLANE, [(0, 1), (1, 0)]))
        owns.append(correlate(own_block[:, first : first + half], plane_blocks, inverse_count))
    plane = lax.axis_index(PLANE)
    span = plane_blocks.shape[0]
    whole = jnp.zeros((2, feeds, 2 * span, width), jnp.float32)
    for index, (first, _) in enumerate(spans_of):
        whole = lax.dynamic_update_slice(whole, owns[index], (0, 0, plane * span, first))
        whole = lax.dynamic_update_slice(
            whole, others[index], (0, 0, (1 - plane) * span, first)
        )
    return whole


def solution(mesh):
    chan_axes, blk_axes = mesh.devices.shape
    split = jax.sharding.Mesh(
        mesh.devices.reshape(2, chan_axes // 2, 2, 4, blk_axes // 8), CHAN + BLK
    )
    placed = (P(BLK, CHAN), P())
    return jax.shard_map(
        on_device,
        mesh=split,
        in_specs=placed,
        out_specs=P(None, BLK, None, CHAN),
        check_vma=False,
    )
```

```python
import math

import jax
import jax.numpy as jnp
from jax import lax
from jax.experimental.layout import Layout, with_layout_constraint
from jax.sharding import PartitionSpec as P

TAPS = 8
L = 4096
C = 2048
ROOT = 64
CHAN = ("z_lo", "core")
PLANE = "z_hi"
WITHIN = ("y", "x")
BLK = (PLANE,) + WITHIN


def shifted(value, axis, steps):
    count = lax.axis_size(axis)
    leading, last = (max(0, -steps), min(count, count - steps))
    return lax.ppermute(value, axis, [(source, source + steps) for source in range(leading, last)])


def turn(rows, columns, length):
    phase_index = jnp.arange(rows, dtype=jnp.int32)[:, None] * jnp.arange(
        columns, dtype=jnp.int32
    )[None, :] % length
    angles = phase_index.astype(jnp.float32) * (2.0 * math.pi / length)
    return jnp.cos(angles), -jnp.sin(angles)


def spectra_of(frames, groups):
    rows = frames.shape[0]
    exact = lax.Precision.HIGHEST
    first_cos, first_sin = turn(ROOT, ROOT, ROOT)
    first_table = jnp.concatenate([first_cos, first_sin], axis=1) * (1.0 / math.sqrt(L))
    split = frames.reshape(rows, ROOT, ROOT)
    stage = jnp.einsum(
        "rab,ak->rkb", split, first_table, precision=exact, preferred_element_type=jnp.float32
    )
    stage_real, stage_imag = stage[:, :ROOT], stage[:, ROOT:]
    twiddle_real, twiddle_imag = turn(ROOT, ROOT, L)
    turned_real = stage_real * twiddle_real - stage_imag * twiddle_imag
    turned_imag = stage_real * twiddle_imag + stage_imag * twiddle_real
    kept = C // ROOT
    second_cos, second_sin = turn(ROOT, kept, ROOT)
    second_table = jnp.concatenate(
        [
            jnp.concatenate([second_cos, second_sin], axis=1),
            jnp.concatenate([-second_sin, second_cos], axis=1),
        ],
        axis=0,
    )
    turned = jnp.concatenate([turned_real, turned_imag], axis=2)
    product = jnp.einsum(
        "rkb,bm->rkm", turned, second_table, precision=exact, preferred_element_type=jnp.float32
    )
    per_group = kept // groups
    product = product.reshape(rows, ROOT, 2, groups, per_group)
    return product.transpose(3, 0, 2, 4, 1).reshape(groups, rows, 2, per_group * ROOT)


def correlate(own_block, every_block, inverse_count):
    real_part, imag_part = own_block[:, :, :, 0], own_block[:, :, :, 1]
    paired = jnp.stack(
        [jnp.stack([real_part, imag_part], axis=3), jnp.stack([imag_part, -real_part], axis=3)]
    )
    left = paired.reshape((2,) + own_block.shape[:2] + (-1,))
    products = jnp.einsum("rick,jck->rijc", left, every_block, preferred_element_type=jnp.float32)
    return products * inverse_count


def corner_turn(spectra):
    count = lax.axis_size(CHAN)
    me = lax.axis_index(CHAN)
    planes = []
    for flip in range(2):
        pieces = []
        for steps in range(count):
            outgoing = lax.dynamic_index_in_dim(
                spectra, (me + steps) % count, axis=1, keepdims=False
            )
            if steps or flip:
                pairs = [
                    (source * 2 + plane, ((source + steps) % count) * 2 + (plane ^ flip))
                    for source in range(count)
                    for plane in range(2)
                ]
                outgoing = lax.ppermute(outgoing, CHAN + (PLANE,), pairs)
            pieces.append(outgoing)
        planes.append(jnp.stack(pieces, axis=1))
    return planes


def on_device(voltages, fir_taps):
    feed_count = voltages.shape[0]
    frame_count = voltages.shape[1] // L
    groups = lax.axis_size(CHAN)
    own_frames = voltages.reshape(feed_count, frame_count, L)
    last_frames = own_frames[:, frame_count - (TAPS - 1) :, :]
    earlier = shifted(last_frames, CHAN, 1)
    extended = jnp.concatenate([earlier, own_frames], axis=1)
    filtered = jnp.zeros((feed_count, frame_count, L), jnp.float32)
    for tap_index in range(TAPS):
        filtered = filtered + fir_taps[tap_index][None, None, :] * extended[
            :, tap_index : tap_index + frame_count, :
        ].astype(jnp.float32)
    frame_rows = filtered.reshape(feed_count * frame_count, L)
    spectra = spectra_of(frame_rows, groups).astype(jnp.bfloat16)
    width = spectra.shape[-1]
    spectra = spectra.reshape(groups, feed_count, frame_count, 2, width).transpose(1, 0, 3, 2, 4)
    own_block, partner_block = corner_turn(spectra)
    inverse_count = 1.0 / (groups * frame_count)
    feeds, spans, parts, frames, width = own_block.shape

    own_block = own_block.transpose(0, 4, 1, 2, 3)
    partner_block = partner_block.transpose(0, 4, 1, 2, 3)
    row_major = Layout(major_to_minor=tuple(range(4)))
    split = width * 3 // 4
    spans_of = [(0, split), (split, width - split)]
    owns, others, sent = [], [], []
    for first, half in spans_of:
        local = with_layout_constraint(
            own_block[:, first : first + half].reshape(1, feeds, half, spans * parts * frames),
            row_major,
        )
        gathered = with_layout_constraint(
            lax.all_gather(local, WITHIN, axis=0, tiled=True), row_major
        )
        plane_blocks = gathered.reshape((-1,) + gathered.shape[2:])
        if owns:
            plane_blocks, owns[0], _ = lax.optimization_barrier(
                (plane_blocks, owns[0], sent[0])
            )
        partner_part = correlate(
            partner_block[:, first : first + half], plane_blocks, inverse_count
        )
        sent.append(partner_part)
        others.append(lax.ppermute(partner_part, PLANE, [(0, 1), (1, 0)]))
        owns.append(correlate(own_block[:, first : first + half], plane_blocks, inverse_count))
    plane = lax.axis_index(PLANE)
    span = plane_blocks.shape[0]
    whole = jnp.zeros((2, feeds, 2 * span, width), jnp.float32)
    for index, (first, _) in enumerate(spans_of):
        whole = lax.dynamic_update_slice(whole, owns[index], (0, 0, plane * span, first))
        whole = lax.dynamic_update_slice(
            whole, others[index], (0, 0, (1 - plane) * span, first)
        )
    return whole


def solution(mesh):
    chan_axes, blk_axes = mesh.devices.shape
    split = jax.sharding.Mesh(
        mesh.devices.reshape(2, chan_axes // 2, 2, 4, blk_axes // 8), CHAN + BLK
    )
    placed = (P(BLK, CHAN), P())
    return jax.shard_map(
        on_device,
        mesh=split,
        in_specs=placed,
        out_specs=P(None, BLK, None, CHAN),
        check_vma=False,
    )
```

```python
import math

import jax
import jax.numpy as jnp
from jax import lax
from jax.experimental.layout import Layout, with_layout_constraint
from jax.sharding import PartitionSpec as P

TAPS = 8
L = 4096
C = 2048
ROOT = 64
CHAN = ("z_lo", "core")
PLANE = "z_hi"
WITHIN = ("y", "x")
BLK = (PLANE,) + WITHIN


def shifted(value, axis, steps):
    count = lax.axis_size(axis)
    leading, last = (max(0, -steps), min(count, count - steps))
    return lax.ppermute(value, axis, [(source, source + steps) for source in range(leading, last)])


def turn(rows, columns, length):
    phase_index = jnp.arange(rows, dtype=jnp.int32)[:, None] * jnp.arange(
        columns, dtype=jnp.int32
    )[None, :] % length
    angles = phase_index.astype(jnp.float32) * (2.0 * math.pi / length)
    return jnp.cos(angles), -jnp.sin(angles)


def spectra_of(frames, groups):
    rows = frames.shape[0]
    exact = lax.Precision.HIGHEST
    first_cos, first_sin = turn(ROOT, ROOT, ROOT)
    first_table = jnp.concatenate([first_cos, first_sin], axis=1) * (1.0 / math.sqrt(L))
    split = frames.reshape(rows, ROOT, ROOT)
    stage = jnp.einsum(
        "rab,ak->rkb", split, first_table, precision=exact, preferred_element_type=jnp.float32
    )
    stage_real, stage_imag = stage[:, :ROOT], stage[:, ROOT:]
    twiddle_real, twiddle_imag = turn(ROOT, ROOT, L)
    turned_real = stage_real * twiddle_real - stage_imag * twiddle_imag
    turned_imag = stage_real * twiddle_imag + stage_imag * twiddle_real
    kept = C // ROOT
    second_cos, second_sin = turn(ROOT, kept, ROOT)
    second_table = jnp.concatenate(
        [
            jnp.concatenate([second_cos, second_sin], axis=1),
            jnp.concatenate([-second_sin, second_cos], axis=1),
        ],
        axis=0,
    )
    turned = jnp.concatenate([turned_real, turned_imag], axis=2)
    product = jnp.einsum(
        "rkb,bm->rkm", turned, second_table, precision=exact, preferred_element_type=jnp.float32
    )
    per_group = kept // groups
    product = product.reshape(rows, ROOT, 2, groups, per_group)
    return product.transpose(3, 0, 2, 4, 1).reshape(groups, rows, 2, per_group * ROOT)


def correlate(own_block, every_block, inverse_count):
    real_part, imag_part = own_block[:, :, :, 0], own_block[:, :, :, 1]
    paired = jnp.stack(
        [jnp.stack([real_part, imag_part], axis=3), jnp.stack([imag_part, -real_part], axis=3)]
    )
    left = paired.reshape((2,) + own_block.shape[:2] + (-1,))
    products = jnp.einsum("rick,jck->rijc", left, every_block, preferred_element_type=jnp.float32)
    return products * inverse_count


def corner_turn(spectra):
    count = lax.axis_size(CHAN)
    me = lax.axis_index(CHAN)
    planes = []
    for flip in range(2):
        pieces = []
        for steps in range(count):
            outgoing = lax.dynamic_index_in_dim(
                spectra, (me + steps) % count, axis=1, keepdims=False
            )
            if steps or flip:
                pairs = [
                    (source * 2 + plane, ((source + steps) % count) * 2 + (plane ^ flip))
                    for source in range(count)
                    for plane in range(2)
                ]
                outgoing = lax.ppermute(outgoing, CHAN + (PLANE,), pairs)
            pieces.append(outgoing)
        planes.append(jnp.stack(pieces, axis=1))
    return planes


def on_device(voltages, fir_taps):
    feed_count = voltages.shape[0]
    frame_count = voltages.shape[1] // L
    groups = lax.axis_size(CHAN)
    own_frames = voltages.reshape(feed_count, frame_count, L)
    last_frames = own_frames[:, frame_count - (TAPS - 1) :, :]
    earlier = shifted(last_frames, CHAN, 1)
    extended = jnp.concatenate([earlier, own_frames], axis=1)
    filtered = jnp.zeros((feed_count, frame_count, L), jnp.float32)
    for tap_index in range(TAPS):
        filtered = filtered + fir_taps[tap_index][None, None, :] * extended[
            :, tap_index : tap_index + frame_count, :
        ].astype(jnp.float32)
    frame_rows = filtered.reshape(feed_count * frame_count, L)
    spectra = spectra_of(frame_rows, groups).astype(jnp.bfloat16)
    width = spectra.shape[-1]
    spectra = spectra.reshape(groups, feed_count, frame_count, 2, width).transpose(1, 0, 3, 2, 4)
    own_block, partner_block = corner_turn(spectra)
    inverse_count = 1.0 / (groups * frame_count)
    feeds, spans, parts, frames, width = own_block.shape

    own_block = own_block.transpose(0, 4, 1, 2, 3)
    partner_block = partner_block.transpose(0, 4, 1, 2, 3)
    row_major = Layout(major_to_minor=tuple(range(4)))
    half = width // 2
    owns, others, sent = [], [], []
    for first in (0, half):
        local = with_layout_constraint(
            own_block[:, first : first + half].reshape(1, feeds, half, spans * parts * frames),
            row_major,
        )
        gathered = with_layout_constraint(
            lax.all_gather(local, WITHIN, axis=0, tiled=True), row_major
        )
        plane_blocks = gathered.reshape((-1,) + gathered.shape[2:])
        if owns:
            plane_blocks, owns[0], _ = lax.optimization_barrier(
                (plane_blocks, owns[0], tuple(sent))
            )
        quarter = half // 2
        for offset in (0, quarter):
            partner_part = correlate(
                partner_block[:, first + offset : first + offset + quarter],
                plane_blocks[:, offset : offset + quarter],
                inverse_count,
            )
            sent.append(partner_part)
            others.append(lax.ppermute(partner_part, PLANE, [(0, 1), (1, 0)]))
        owns.append(correlate(own_block[:, first : first + half], plane_blocks, inverse_count))
    plane = lax.axis_index(PLANE)
    span = plane_blocks.shape[0]
    whole = jnp.zeros((2, feeds, 2 * span, width), jnp.float32)
    for index in range(2):
        whole = lax.dynamic_update_slice(whole, owns[index], (0, 0, plane * span, index * half))
    for index, other_part in enumerate(others):
        whole = lax.dynamic_update_slice(
            whole, other_part, (0, 0, (1 - plane) * span, index * quarter)
        )
    return whole


def solution(mesh):
    chan_axes, blk_axes = mesh.devices.shape
    split = jax.sharding.Mesh(
        mesh.devices.reshape(2, chan_axes // 2, 2, 4, blk_axes // 8), CHAN + BLK
    )
    placed = (P(BLK, CHAN), P())
    return jax.shard_map(
        on_device,
        mesh=split,
        in_specs=placed,
        out_specs=P(None, BLK, None, CHAN),
        check_vma=False,
    )
```

```python
import math

import jax
import jax.numpy as jnp
from jax import lax
from jax.experimental.layout import Layout, with_layout_constraint
from jax.sharding import PartitionSpec as P

TAPS = 8
L = 4096
C = 2048
ROOT = 64
CHAN = ("z_lo", "core")
PLANE = "z_hi"
WITHIN = ("y", "x")
BLK = (PLANE,) + WITHIN


def shifted(value, axis, steps):
    count = lax.axis_size(axis)
    leading, last = (max(0, -steps), min(count, count - steps))
    return lax.ppermute(value, axis, [(source, source + steps) for source in range(leading, last)])


def turn(rows, columns, length):
    phase_index = jnp.arange(rows, dtype=jnp.int32)[:, None] * jnp.arange(
        columns, dtype=jnp.int32
    )[None, :] % length
    angles = phase_index.astype(jnp.float32) * (2.0 * math.pi / length)
    return jnp.cos(angles), -jnp.sin(angles)


def spectra_of(frames, groups):
    rows = frames.shape[0]
    exact = lax.Precision.HIGHEST
    first_cos, first_sin = turn(ROOT, ROOT, ROOT)
    first_table = jnp.concatenate([first_cos, first_sin], axis=1) * (1.0 / math.sqrt(L))
    split = frames.reshape(rows, ROOT, ROOT)
    stage = jnp.einsum(
        "rab,ak->rkb", split, first_table, precision=exact, preferred_element_type=jnp.float32
    )
    stage_real, stage_imag = stage[:, :ROOT], stage[:, ROOT:]
    twiddle_real, twiddle_imag = turn(ROOT, ROOT, L)
    turned_real = stage_real * twiddle_real - stage_imag * twiddle_imag
    turned_imag = stage_real * twiddle_imag + stage_imag * twiddle_real
    kept = C // ROOT
    second_cos, second_sin = turn(ROOT, kept, ROOT)
    second_table = jnp.concatenate(
        [
            jnp.concatenate([second_cos, second_sin], axis=1),
            jnp.concatenate([-second_sin, second_cos], axis=1),
        ],
        axis=0,
    )
    turned = jnp.concatenate([turned_real, turned_imag], axis=2)
    product = jnp.einsum(
        "rkb,bm->rkm", turned, second_table, precision=exact, preferred_element_type=jnp.float32
    )
    per_group = kept // groups
    product = product.reshape(rows, ROOT, 2, groups, per_group)
    return product.transpose(3, 0, 2, 4, 1).reshape(groups, rows, 2, per_group * ROOT)


def correlate(own_block, every_block, inverse_count):
    real_part, imag_part = own_block[:, :, :, 0], own_block[:, :, :, 1]
    paired = jnp.stack(
        [jnp.stack([real_part, imag_part], axis=3), jnp.stack([imag_part, -real_part], axis=3)]
    )
    left = paired.reshape((2,) + own_block.shape[:2] + (-1,))
    products = jnp.einsum("rick,jck->rijc", left, every_block, preferred_element_type=jnp.float32)
    return products * inverse_count


def corner_turn(spectra):
    count = lax.axis_size(CHAN)
    me = lax.axis_index(CHAN)
    planes = []
    for flip in range(2):
        pieces = []
        for steps in range(count):
            outgoing = lax.dynamic_index_in_dim(
                spectra, (me + steps) % count, axis=1, keepdims=False
            )
            if steps or flip:
                pairs = [
                    (source * 2 + plane, ((source + steps) % count) * 2 + (plane ^ flip))
                    for source in range(count)
                    for plane in range(2)
                ]
                outgoing = lax.ppermute(outgoing, CHAN + (PLANE,), pairs)
            pieces.append(outgoing)
        planes.append(jnp.stack(pieces, axis=1))
    return planes


def on_device(voltages, fir_taps):
    feed_count = voltages.shape[0]
    frame_count = voltages.shape[1] // L
    groups = lax.axis_size(CHAN)
    own_frames = voltages.reshape(feed_count, frame_count, L)
    last_frames = own_frames[:, frame_count - (TAPS - 1) :, :]
    earlier = shifted(last_frames, CHAN, 1)
    extended = jnp.concatenate([earlier, own_frames], axis=1)
    filtered = jnp.zeros((feed_count, frame_count, L), jnp.float32)
    for tap_index in range(TAPS):
        filtered = filtered + fir_taps[tap_index][None, None, :] * extended[
            :, tap_index : tap_index + frame_count, :
        ].astype(jnp.float32)
    frame_rows = filtered.reshape(feed_count * frame_count, L)
    spectra = spectra_of(frame_rows, groups).astype(jnp.bfloat16)
    width = spectra.shape[-1]
    spectra = spectra.reshape(groups, feed_count, frame_count, 2, width).transpose(1, 0, 3, 2, 4)
    own_block, partner_block = corner_turn(spectra)
    inverse_count = 1.0 / (groups * frame_count)
    feeds, spans, parts, frames, width = own_block.shape

    own_block = own_block.transpose(0, 4, 1, 2, 3)
    partner_block = partner_block.transpose(0, 4, 1, 2, 3)
    row_major = Layout(major_to_minor=tuple(range(4)))
    split = width * 3 // 4
    spans_of = [(0, split), (split, width - split)]
    quarter = width // 4
    owns, others, sent = [], [], []
    for first, half in spans_of:
        local = with_layout_constraint(
            own_block[:, first : first + half].reshape(1, feeds, half, spans * parts * frames),
            row_major,
        )
        gathered = with_layout_constraint(
            lax.all_gather(local, WITHIN, axis=0, tiled=True), row_major
        )
        plane_blocks = gathered.reshape((-1,) + gathered.shape[2:])
        if owns:
            plane_blocks, owns[0], _ = lax.optimization_barrier(
                (plane_blocks, owns[0], tuple(sent))
            )
        for offset in range(0, half, quarter):
            partner_part = correlate(
                partner_block[:, first + offset : first + offset + quarter],
                plane_blocks[:, offset : offset + quarter],
                inverse_count,
            )
            sent.append(partner_part)
            others.append(lax.ppermute(partner_part, PLANE, [(0, 1), (1, 0)]))
        owns.append(correlate(own_block[:, first : first + half], plane_blocks, inverse_count))
    plane = lax.axis_index(PLANE)
    span = plane_blocks.shape[0]
    whole = jnp.zeros((2, feeds, 2 * span, width), jnp.float32)
    for index, (first, _) in enumerate(spans_of):
        whole = lax.dynamic_update_slice(whole, owns[index], (0, 0, plane * span, first))
    for index, other_part in enumerate(others):
        whole = lax.dynamic_update_slice(
            whole, other_part, (0, 0, (1 - plane) * span, index * quarter)
        )
    return whole


def solution(mesh):
    chan_axes, blk_axes = mesh.devices.shape
    split = jax.sharding.Mesh(
        mesh.devices.reshape(2, chan_axes // 2, 2, 4, blk_axes // 8), CHAN + BLK
    )
    placed = (P(BLK, CHAN), P())
    return jax.shard_map(
        on_device,
        mesh=split,
        in_specs=placed,
        out_specs=P(None, BLK, None, CHAN),
        check_vma=False,
    )
```
